256 devices in a mesh: seq: 64 (over z_hi, y, x, core), tp: 4 (over z_lo).
Axes of the slice: x: 4, y: 4, z: 8 (z_hi: 2, z_lo: 4; z = z_hi * 4 + z_lo), core: 2. Of those that a mesh axis runs over, the one named last changes fastest.
Arguments:
- hidden_in: bfloat16 [16384, 2048], P(('seq', 'tp')), may hold values from -6 to 6
- attention_gain: float32 [2048], replicated, may hold values from 0.1 to 1.9
- attention_trainer_copy: float32 [2048, 5120], P(('seq', 'tp')), may hold values from -0.125 to 0.125
- query_gain: float32 [128], replicated, may hold values from 0.1 to 1.9
- key_gain: float32 [128], replicated, may hold values from 0.1 to 1.9
- output_proj: bfloat16 [4096, 2048], P('tp'), may hold values from -0.09375 to 0.09375
- post_gain: float32 [2048], replicated, may hold values from 0.1 to 1.9
- router_weight: bfloat16 [2048, 128], replicated, may hold values from -0.125 to 0.125
- gate_up_master: float32 [128, 2048, 1536], P(None, ('seq', 'tp')), may hold values from -0.125 to 0.125
- down_weight: bfloat16 [128, 768, 2048], P('seq', 'tp'), may hold values from -0.21875 to 0.21875
- routes: int32 [16384, 8], P(('seq', 'tp')), may hold values from 0 to 127, all different within a row; in each aligned block of 64 rows (0 to 63, 64 to 127, ...) at most 8 rows name the same one
- lengths: int32 [64], P('seq'), may hold values from 1 to 256, 8192 in all
- page_table: int32 [64, 2], P('seq'), may hold values from 0 to 3, as said below
Outputs:
- hidden_leaving: bfloat16 [16384, 2048], P(('seq', 'tp'))
- cache_pages: bfloat16 [256, 2, 4, 128, 128], P('seq', None, 'tp')
The draws below stay inside these ranges and needn't reach their ends.
Inputs may be any that keep to these rules, and one draw needn't show every extreme that they name: `routes`: each row names 8 different experts. In each aligned block of 64 rows (the rows of one device) no expert is named by more than 8 rows, a bound that some block reaches. `lengths`: some prompt has exactly 256 live positions. `page_table`: the 2 slots of one prompt are distinct.
All inputs are finite; a program needn't handle non-finite values. No bound on the sum of `lengths` on one device may be relied on, other than what follows from the above.
Results may differ from the reference program's by a relative error of at most 0.0085.
Values may be sent and summed in bfloat16 or wider, within the bound.
No kernel may reach another device: no remote copies, remote signals or barrier semaphores. Data moves between devices by JAX's collectives and lax.ppermute only.
A program may use at most 128 MiB of HBM per device.

```python
import math
import jax
import jax.numpy as jnp
import numpy as np
from jax import lax

D = 2048
QUERY_HEADS = 32
KEY_VALUE_HEADS = 4
HEAD_SIZE = 128
FF = 768
TOPK = 8
PAGE_POSITIONS = 128
PADDED_LENGTH = 256
E = 128
QKVW = 5120
CAP = 8
PROMPTS = 64
TOKENS = 16384
PROMPT_PAGES = 2
PROMPT_SLOTS = 4
CACHE_SLOTS = 256
N_SEQ = 64
N_TP = 4


def draw_page_table(key, part):
    keys_all = jax.random.split(jax.random.fold_in(key, 7), PROMPTS)

    def one_prompt(prompt_key):
        return jax.random.permutation(prompt_key, PROMPT_SLOTS)[:PROMPT_PAGES]
    return jax.vmap(one_prompt)(keys_all).astype(jnp.int32)


def shard_levels(key, extent, shards, low, high):
    def one(axis_at, parts):
        steps = jax.random.uniform(jax.random.fold_in(jax.random.fold_in(key, 6), axis_at), (parts,), jnp.float32, low / len(shards), high / len(shards))
        return jnp.repeat(jnp.exp(steps), extent[axis_at] // parts).reshape((-1,) + (1,) * (len(extent) - axis_at - 1))

    level = one(*shards[0])
    for cut in shards[1:]:
        level = level * one(*cut)
    return level


def length_profile(count, total, bound, lean):
    loads = [(1 << 20) // math.isqrt(rank ** lean) + 1 for rank in range(2, count + 1)]
    spare, given = total - bound - (count - 1), [1] * (count - 1)
    while spare > 0:
        free = [i for i in range(count - 1) if given[i] < bound]
        whole, budget = sum([loads[i] for i in free]), spare
        for i in free:
            addition = min(bound - given[i], max(1, budget * loads[i] // whole), spare)
            given[i] = given[i] + addition
            spare = spare - addition
    return np.array([bound] + given)


def uneven(stream_key, count, total, reach, lean):
    if count == 2:
        one = jax.random.randint(stream_key, (), max(1, total - reach), min(reach, total - 1) + 1)
        return jnp.stack([one, total - one])
    sizes = jnp.asarray(length_profile(count, total, reach, lean), jnp.int32)
    couples = (count - 1) // 2
    source_of, receiver = sizes[1:1 + 2 * couples:2], sizes[2:2 + 2 * couples:2]
    room = jnp.minimum(source_of - 1, reach - receiver)
    passed = jax.random.randint(jax.random.fold_in(stream_key, 1), (couples,), 0, 1 << 20) % (room + 1)
    sizes = sizes.at[1:1 + 2 * couples:2].set(source_of - passed).at[2:2 + 2 * couples:2].set(receiver + passed)
    return sizes[jax.random.permutation(jax.random.fold_in(stream_key, 2), count)]


def assign_block(own_key, own, number, rows, count, top, reach, lean):
    order = jax.random.permutation(own_key, count)
    crowded, ordinary = portions_of(count, rows * top, reach, lean, True), portions_of(count, rows * top, reach, lean, False)
    places = jnp.arange(count)

    def named(tallies, turn):
        used = int((tallies > 0).sum())
        fixed = max(1, used // 4)
        shifted = fixed + (places - fixed + turn * (used - fixed)) % max(1, count - fixed)
        return jnp.zeros((count,), jnp.int32).at[order[jnp.where(places < fixed, places, shifted)]].set(jnp.asarray(tallies, jnp.int32))

    tallies = jnp.where(number % 4 == 0, named(crowded, number // 4), named(ordinary, number - number // 4 - 1))
    mixed = jax.random.permutation(jax.random.fold_in(own, 3), count)
    giver, receiver = mixed[0:count // 2 * 2:2], mixed[1:count // 2 * 2:2]
    margin = jnp.minimum(tallies[giver] - 1, reach - tallies[receiver]) // 2
    margin = jnp.where((giver == order[0]) | (receiver == order[0]) | (tallies[receiver] == 0), 0, jnp.maximum(margin, 0))
    shifted = jax.random.randint(jax.random.fold_in(own, 4), (count // 2,), 0, 1 << 20) % (margin + 1)
    tallies = tallies.at[giver].add(-shifted).at[receiver].add(shifted)
    items = jnp.searchsorted(jnp.cumsum(tallies), jnp.arange(rows * top), side="right").astype(jnp.int32)
    listing = items.reshape(top, rows).T
    listing = listing[jax.random.permutation(jax.random.fold_in(own, 1), rows)]
    turn = jax.random.randint(jax.random.fold_in(own, 2), (rows, 1), 0, top)
    return jnp.take_along_axis(listing, (jnp.arange(top)[None, :] + turn) % top, axis=1)


def portions_of(number_of, total, limit, slope, full):
    portions = [(1 << 20) // math.isqrt(grade ** slope) + 1 for grade in range(1, number_of + 1)]
    largest = limit if full else min(limit, max(-(-total // number_of), total * portions[0] // sum(portions)))
    least = 1 if total - largest >= number_of - 1 else 0
    holding, surplus = [largest] + [least] * (number_of - 1), total - largest - least * (number_of - 1)
    while surplus > 0:
        free = [i for i in range(1, number_of) if holding[i] < largest] or [i for i in range(1, number_of) if holding[i] < limit]
        pool, remaining = sum([portions[i] for i in free]), surplus
        for i in free:
            addition = min(limit - holding[i], max(1, remaining * portions[i] // pool), surplus)
            holding[i] = holding[i] + addition
            surplus = surplus - addition
    return np.array(holding)


def scatter_about(rng, dims, width, limit, pieces=(), held_as=jnp.bfloat16):
    drawn = jax.random.normal(rng, dims, jnp.float32) * width
    if len(pieces) > 0:
        drawn = shard_levels(rng, dims, pieces, -0.22, 0.18) * drawn
    return jnp.clip(drawn, min=-limit, max=limit).astype(held_as)


def setup_inputs(seed: int = 0) -> dict:
    key_of = jax.random.split(jax.random.key(seed), 14)
    hidden_in = scatter_about(key_of[0], (TOKENS, D), 1.0, 6.0, ((0, 256),))
    attention_gain = jnp.clip(1.0 + 0.18 * jax.random.normal(key_of[1], (D,), jnp.float32), 0.1, 1.9)
    attention_trainer_copy = scatter_about(key_of[2], (D, QKVW), D ** -0.5, 0.125, ((0, 256),), jnp.float32)
    query_gain = jnp.clip(1.0 + 0.18 * jax.random.normal(key_of[3], (HEAD_SIZE,), jnp.float32), 0.1, 1.9)
    key_gain = jnp.clip(1.0 + 0.18 * jax.random.normal(key_of[4], (HEAD_SIZE,), jnp.float32), 0.1, 1.9)
    output_proj = scatter_about(key_of[5], (QUERY_HEADS * HEAD_SIZE, D), (QUERY_HEADS * HEAD_SIZE) ** -0.5, 0.09375, ((0, 4),))
    post_gain = jnp.clip(1.0 + 0.18 * jax.random.normal(key_of[6], (D,), jnp.float32), 0.1, 1.9)
    router_weight = scatter_about(key_of[7], (D, E), D ** -0.5, 0.125)
    gate_up_master = scatter_about(key_of[8], (E, D, 2 * FF), D ** -0.5, 0.125, ((1, 256),), jnp.float32)
    down_weight = scatter_about(key_of[9], (E, FF, D), FF ** -0.5, 0.21875, ((0, 64), (1, 4)))
    routes_keys = jax.random.split(jax.random.fold_in(key_of[10], 1), TOKENS // (PADDED_LENGTH // N_TP))
    routes_turns = jax.random.permutation(jax.random.fold_in(key_of[10], 3), TOKENS // (PADDED_LENGTH // N_TP))
    routes = jax.vmap(lambda own, number: assign_block(jax.random.fold_in(key_of[10], 2), own, number, PADDED_LENGTH // N_TP, E, TOPK, CAP, 1))(routes_keys, routes_turns).reshape((TOKENS, TOPK))
    lengths = uneven(key_of[11], PROMPTS, PROMPTS * PADDED_LENGTH // 2, PADDED_LENGTH, 2).astype(jnp.int32)
    page_table = draw_page_table(jax.random.fold_in(key_of[13], 71), 0)
    return {"hidden_in": hidden_in, "attention_gain": attention_gain, "attention_trainer_copy": attention_trainer_copy, "query_gain": query_gain, "key_gain": key_gain, "output_proj": output_proj, "post_gain": post_gain, "router_weight": router_weight, "gate_up_master": gate_up_master, "down_weight": down_weight, "routes": routes, "lengths": lengths, "page_table": page_table}


EPS = 1e-06
THETA = 1000000.0

def rms_scale(values, gain):
    return values * lax.rsqrt(lax.optimization_barrier(jnp.mean(values * values, axis=-1, keepdims=True)) + EPS) * gain

def rotate(values, positions):
    half_dim = values.shape[-1] // 2
    frequency = THETA ** (-2.0 * jnp.arange(half_dim, dtype=jnp.float32) / values.shape[-1])
    angles = positions.astype(jnp.float32)[:, None] * frequency[None, :]
    cosine = jnp.cos(angles)[:, None, :]
    sine = jnp.sin(angles)[:, None, :]
    first_half = values[..., :half_dim]
    second_half = values[..., half_dim:]
    return jnp.concatenate([first_half * cosine - second_half * sine, second_half * cosine + first_half * sine], axis=-1)

def attend_prompt(query_rows, keys_rotated, values_in, prompt_length):
    column_span = query_rows.shape[0]
    scores = jnp.einsum('qhgd,khd->hgqk', query_rows.astype(jnp.float32), keys_rotated.astype(jnp.float32)) / math.sqrt(query_rows.shape[-1])
    places = jnp.arange(column_span)
    allowed = (places[None, :] <= places[:, None]) & (places[None, :] < prompt_length)
    weights = jnp.where(allowed, jnp.exp(scores), 0.0)
    probs = (weights / lax.optimization_barrier(jnp.sum(weights, axis=-1, keepdims=True))).astype(jnp.bfloat16)
    context_rows = jnp.einsum('hgqk,khd->qhgd', probs.astype(jnp.float32), values_in.astype(jnp.float32))
    return context_rows.astype(jnp.bfloat16).reshape(column_span, -1)

def reference(hidden_in, attention_gain, attention_trainer_copy, query_gain, key_gain, output_proj, post_gain, router_weight, gate_up_master, down_weight, routes, lengths, page_table):
    query_group_width = QUERY_HEADS // KEY_VALUE_HEADS
    inputs = hidden_in.astype(jnp.float32)
    normed = rms_scale(inputs, attention_gain).astype(jnp.bfloat16)
    attention_weight = lax.optimization_barrier(attention_trainer_copy.astype(jnp.bfloat16))
    projected_rows = jnp.einsum('td,dc->tc', normed.astype(jnp.float32), attention_weight.astype(jnp.float32))
    positions = jnp.arange(PADDED_LENGTH)
    query_all = projected_rows[:, :QUERY_HEADS * HEAD_SIZE].reshape(N_SEQ, PADDED_LENGTH, QUERY_HEADS, HEAD_SIZE)
    key_gathered = projected_rows[:, QUERY_HEADS * HEAD_SIZE:(QUERY_HEADS + KEY_VALUE_HEADS) * HEAD_SIZE].reshape(N_SEQ, PADDED_LENGTH, KEY_VALUE_HEADS, HEAD_SIZE)
    value_gathered = projected_rows[:, (QUERY_HEADS + KEY_VALUE_HEADS) * HEAD_SIZE:].reshape(N_SEQ, PADDED_LENGTH, KEY_VALUE_HEADS, HEAD_SIZE).astype(jnp.bfloat16)
    query_all = jax.vmap(lambda prompt_block: rotate(rms_scale(prompt_block, query_gain), positions))(query_all).astype(jnp.bfloat16)
    key_gathered = jax.vmap(lambda prompt_block: rotate(rms_scale(prompt_block, key_gain), positions))(key_gathered).astype(jnp.bfloat16)

    def one_prompt(items):
        query_local, key_local, value_local, prompt_length = items
        return attend_prompt(query_local.reshape(PADDED_LENGTH, KEY_VALUE_HEADS, query_group_width, HEAD_SIZE), key_local, value_local, prompt_length)
    context_rows = lax.map(one_prompt, (query_all, key_gathered, value_gathered, lengths)).reshape(TOKENS, QUERY_HEADS * HEAD_SIZE)
    after_attn = inputs + jnp.einsum('tc,cd->td', context_rows.astype(jnp.float32), output_proj.astype(jnp.float32))
    mixed = rms_scale(after_attn, post_gain).astype(jnp.bfloat16)
    logits = jnp.einsum('td,de->te', mixed.astype(jnp.float32), router_weight.astype(jnp.float32))
    chosen = jnp.take_along_axis(logits, routes, axis=1)
    raised = jnp.exp(chosen)
    gates = raised / lax.optimization_barrier(jnp.sum(raised, axis=1, keepdims=True))
    pair_count = TOKENS * TOPK
    most_rows = N_SEQ * N_TP * CAP
    quarter_units = FF // N_TP
    flat_expert = routes.reshape(-1).astype(jnp.int32)
    order = jnp.argsort(flat_expert, stable=True).astype(jnp.int32)
    counts = lax.optimization_barrier(jnp.sum((flat_expert[:, None] == jnp.arange(E, dtype=jnp.int32)[None, :]).astype(jnp.int32), axis=0)).astype(jnp.int32)
    starts = (jnp.cumsum(counts) - counts).astype(jnp.int32)
    token_sorted = jnp.concatenate([order // TOPK, jnp.zeros((most_rows,), jnp.int32)]).astype(jnp.int32)

    def one_expert(expert):
        picked = lax.dynamic_slice_in_dim(token_sorted, starts[expert], most_rows)
        expert_rows = mixed[picked]
        weight_here = lax.optimization_barrier(gate_up_master[expert].astype(jnp.bfloat16))
        both = jnp.einsum('md,df->mf', expert_rows.astype(jnp.float32), weight_here.astype(jnp.float32))
        units = (jax.nn.silu(both[:, :FF]) * both[:, FF:]).astype(jnp.bfloat16)
        partial_sums = jnp.einsum('mqf,qfd->qmd', units.reshape(most_rows, N_TP, quarter_units).astype(jnp.float32), down_weight[expert].reshape(N_TP, quarter_units, D).astype(jnp.float32))
        rounded = lax.optimization_barrier(partial_sums.astype(jnp.bfloat16))
        return lax.optimization_barrier(jnp.sum(rounded.astype(jnp.float32), axis=0)).astype(jnp.bfloat16)
    expert_table = lax.map(one_expert, jnp.arange(E, dtype=jnp.int32))
    sorted_expert = flat_expert[order]
    offsets = (jnp.arange(pair_count, dtype=jnp.int32) - starts[sorted_expert]).astype(jnp.int32)
    sorted_out = expert_table[sorted_expert, offsets]
    expert_out = jnp.zeros((pair_count, D), jnp.bfloat16).at[order].set(sorted_out)
    combined = lax.optimization_barrier(jnp.sum(gates[:, :, None] * expert_out.reshape(TOKENS, TOPK, D).astype(jnp.float32), axis=1))
    live_rows = jnp.tile(positions, N_SEQ) < jnp.repeat(lengths, PADDED_LENGTH)
    hidden_leaving = jnp.where(live_rows[:, None], after_attn + combined, 0.0).astype(jnp.bfloat16)
    live = (positions[None, :] < lengths[:, None])[:, :, None, None]
    zero_value = jnp.zeros((), jnp.bfloat16)
    keys_kept = jnp.where(live, key_gathered, zero_value)
    values_kept = jnp.where(live, value_gathered, zero_value)
    prompt_pages = jnp.stack([keys_kept, values_kept], axis=2)
    prompt_pages = prompt_pages.reshape(N_SEQ, PROMPT_PAGES, PAGE_POSITIONS, 2, KEY_VALUE_HEADS, HEAD_SIZE).transpose(0, 1, 3, 4, 2, 5)
    paged_cache = jnp.zeros((N_SEQ, PROMPT_SLOTS, 2, KEY_VALUE_HEADS, PAGE_POSITIONS, HEAD_SIZE), jnp.bfloat16)
    paged_cache = paged_cache.at[jnp.arange(N_SEQ, dtype=jnp.int32)[:, None], page_table].set(prompt_pages)
    return (hidden_leaving, paged_cache.reshape(CACHE_SLOTS, 2, KEY_VALUE_HEADS, PAGE_POSITIONS, HEAD_SIZE))
```

```python
import functools
import math

import jax
import jax.numpy as jnp
from jax import lax
from jax.sharding import Mesh, PartitionSpec as P

QUERY_HEADS = 32
KEY_VALUE_HEADS = 4
HEAD_SIZE = 128
FF = 768
TOPK = 8
PAGE_POSITIONS = 128


EPS = 1e-06
THETA = 1000000.0


def laid_out(pieces, dim):
    pieces = jnp.moveaxis(pieces, 0, dim)
    lengths = pieces.shape
    return pieces.reshape(*lengths[:dim], lengths[dim] * lengths[dim + 1], *lengths[dim + 2 :])


def from_everyone(array, axis):
    peers = lax.axis_size(axis)
    return lax.all_to_all(
        jnp.broadcast_to(array[None], (peers, *array.shape)), axis, 0, 0, tiled=True
    )


def collect(array, axis, dim):
    return laid_out(from_everyone(array, axis), dim)


def in_blocks(array, dim, peers):
    lengths = array.shape
    pieces = array.reshape(*lengths[:dim], peers, lengths[dim] // peers, *lengths[dim + 1 :])
    return jnp.moveaxis(pieces, dim, 0)


def summed_on_arrival(array, axis, dim):
    peers = lax.axis_size(axis)
    pieces = lax.all_to_all(in_blocks(array, dim, peers), axis, 0, 0, tiled=True)
    return jnp.sum(pieces.astype(jnp.float32), axis=0)


def rms_scale(values, gain):
    return values * lax.rsqrt(jnp.mean(values * values, axis=-1, keepdims=True) + EPS) * gain


def rotate(values, positions):
    half_dim = values.shape[-1] // 2
    frequency = THETA ** (-2.0 * jnp.arange(half_dim, dtype=jnp.float32) / values.shape[-1])
    angles = positions.astype(jnp.float32)[:, None] * frequency[None, :]
    cosine = jnp.cos(angles)[:, None, :]
    sine = jnp.sin(angles)[:, None, :]
    first_half = values[..., :half_dim]
    second_half = values[..., half_dim:]
    return jnp.concatenate(
        [first_half * cosine - second_half * sine, second_half * cosine + first_half * sine],
        axis=-1,
    )


def attend_prompt(query_rows, keys_rotated, values_in, prompt_length):
    column_span = query_rows.shape[0]
    scores = jnp.einsum(
        "qhgd,khd->hgqk", query_rows, keys_rotated, preferred_element_type=jnp.float32
    ) / math.sqrt(query_rows.shape[-1])
    places = jnp.arange(column_span)
    allowed = (places[None, :] <= places[:, None]) & (places[None, :] < prompt_length)
    weights = jnp.where(allowed, jnp.exp(scores), 0.0)
    probs = (weights / jnp.sum(weights, axis=-1, keepdims=True)).astype(jnp.bfloat16)
    context_rows = jnp.einsum(
        "hgqk,khd->qhgd", probs, values_in, preferred_element_type=jnp.float32
    )
    return context_rows.astype(jnp.bfloat16).reshape(column_span, -1)


def regroup(features, seq_count, tensor_parallel_count):
    leading = features.shape[:-1]
    blocks = features.reshape(leading + (seq_count, tensor_parallel_count, -1))
    return jnp.swapaxes(blocks, -3, -2).reshape(leading + (-1,))


def on_device(
    hidden_in,
    attention_gain,
    attention_trainer_copy,
    query_gain,
    key_gain,
    output_proj,
    post_gain,
    router_weight,
    gate_up_master,
    down_weight,
    routes,
    lengths,
    page_table,
    *,
    n_zh,
    n_sub,
    n_tp,
):
    zh = lax.axis_index("zh")
    tp_place = lax.axis_index("tp")
    quarter = hidden_in.shape[0]
    width = hidden_in.shape[1]
    experts_all = router_weight.shape[1]
    half_experts = experts_all // n_zh
    heads_here = QUERY_HEADS // n_tp
    key_value_local = KEY_VALUE_HEADS // n_tp
    ff_half = FF // 2
    ff_quarter = FF // n_tp
    capacity = 2 * 8
    within = ("sub", "tp")
    n_within = n_sub * n_tp

    gate_up_half = gate_up_master.astype(jnp.bfloat16)
    trainer_block = gate_up_half.shape[1]
    gate_up_half = gate_up_half.reshape(n_zh, half_experts, trainer_block, 2 * FF)
    gate_up_half = lax.all_to_all(gate_up_half, "zh", 0, 0, tiled=True)
    pieces = gate_up_half.reshape(n_zh, n_sub, 2, trainer_block, 2 * FF)
    gate_part = pieces[..., :FF].reshape(n_zh, n_sub, 2, trainer_block, 2, ff_half)
    up_part = pieces[..., FF:].reshape(n_zh, n_sub, 2, trainer_block, 2, ff_half)
    pieces = jnp.concatenate([gate_part, up_part], axis=-1)
    pieces = pieces.transpose(1, 4, 2, 0, 3, 5).reshape(n_within, n_zh * trainer_block, FF)
    pieces = lax.all_to_all(pieces, within, 0, 0, tiled=True)
    expert_gate_up = (
        pieces.reshape(n_sub, n_tp, n_zh, trainer_block, FF)
        .transpose(2, 0, 1, 3, 4)
        .reshape(-1, FF)
    )
    parity = tp_place % 2
    kept = lax.dynamic_index_in_dim(down_weight, parity, 0, keepdims=False)
    given = lax.dynamic_index_in_dim(down_weight, 1 - parity, 0, keepdims=False)
    got = lax.ppermute(given, "tp", perm=[(i, i ^ 1) for i in range(n_tp)])
    down_first = jnp.where(parity == 0, kept, got)
    down_second = jnp.where(parity == 0, got, kept)

    prompt_rows = lax.all_gather(hidden_in, "tp", axis=0, tiled=True)
    column_span = prompt_rows.shape[0]
    normed = rms_scale(prompt_rows.astype(jnp.float32), attention_gain).astype(jnp.bfloat16)
    trainer_rows = attention_trainer_copy.shape[0]
    query_cols = attention_trainer_copy[:, : QUERY_HEADS * HEAD_SIZE].reshape(
        trainer_rows, n_tp, heads_here * HEAD_SIZE
    )
    key_columns = attention_trainer_copy[
        :, QUERY_HEADS * HEAD_SIZE : (QUERY_HEADS + KEY_VALUE_HEADS) * HEAD_SIZE
    ].reshape(trainer_rows, n_tp, key_value_local * HEAD_SIZE)
    value_columns = attention_trainer_copy[
        :, (QUERY_HEADS + KEY_VALUE_HEADS) * HEAD_SIZE :
    ].reshape(trainer_rows, n_tp, key_value_local * HEAD_SIZE)
    joined = (
        jnp.concatenate([query_cols, key_columns, value_columns], axis=2)
        .reshape(trainer_rows, -1)
        .astype(jnp.bfloat16)
    )
    head_rows = lax.all_to_all(joined, "tp", split_axis=1, concat_axis=0, tiled=True)
    head_rows = lax.all_gather(head_rows, "zh", axis=0, tiled=True)
    head_rows = lax.all_gather(head_rows, "sub", axis=0, tiled=True)
    seq_block = head_rows.shape[0] // (n_zh * n_sub)
    normed_order = (
        normed.reshape(column_span, n_zh, n_sub, seq_block)
        .transpose(0, 2, 1, 3)
        .reshape(column_span, -1)
    )
    projected_rows = jnp.dot(normed_order, head_rows, preferred_element_type=jnp.float32)
    positions = jnp.arange(column_span)
    query_rows = projected_rows[:, : heads_here * HEAD_SIZE].reshape(
        column_span, heads_here, HEAD_SIZE
    )
    keys_raw = projected_rows[
        :, heads_here * HEAD_SIZE : (heads_here + key_value_local) * HEAD_SIZE
    ].reshape(column_span, key_value_local, HEAD_SIZE)
    values_local_rows = (
        projected_rows[:, (heads_here + key_value_local) * HEAD_SIZE :]
        .reshape(column_span, key_value_local, HEAD_SIZE)
        .astype(jnp.bfloat16)
    )
    query_rows = rotate(rms_scale(query_rows, query_gain), positions).astype(jnp.bfloat16)
    keys_rotated = rotate(rms_scale(keys_raw, key_gain), positions).astype(jnp.bfloat16)
    prompt_length = lengths[0]
    context_rows = attend_prompt(
        query_rows.reshape(column_span, key_value_local, QUERY_HEADS // KEY_VALUE_HEADS, HEAD_SIZE),
        keys_rotated,
        values_local_rows,
        prompt_length,
    )
    attention_sums = summed_on_arrival(
        jnp.dot(context_rows, output_proj, preferred_element_type=jnp.float32).astype(jnp.bfloat16),
        "tp",
        0,
    )
    after_attn = hidden_in.astype(jnp.float32) + attention_sums
    mixed = rms_scale(after_attn, post_gain).astype(jnp.bfloat16)
    logits = jnp.dot(mixed, router_weight, preferred_element_type=jnp.float32)
    chosen = jnp.take_along_axis(logits, routes, axis=1)
    raised = jnp.exp(chosen)
    gates = raised / jnp.sum(raised, axis=1, keepdims=True)

    both_rows = lax.all_gather(mixed, "zh", axis=0, tiled=True)
    both_routes = lax.all_gather(routes, "zh", axis=0, tiled=True)
    both_gates = lax.all_gather(gates, "zh", axis=0, tiled=True)
    row_count = both_rows.shape[0]
    pair_expert = both_routes.reshape(-1)
    local_pair = (pair_expert // half_experts) == zh
    local_expert = pair_expert % half_experts
    hits = (
        (local_expert[:, None] == jnp.arange(half_experts, dtype=jnp.int32)[None, :])
        & local_pair[:, None]
    ).astype(jnp.int32)
    before = jnp.cumsum(hits, axis=0) - hits
    slot_index = jnp.sum(before * hits, axis=1)
    target = jnp.where(local_pair, local_expert * capacity + slot_index, half_experts * capacity)
    outgoing = (
        jnp.zeros((half_experts * capacity, width), jnp.bfloat16)
        .at[target]
        .set(jnp.repeat(both_rows, TOPK, axis=0), mode="drop")
    )
    outgoing = jnp.broadcast_to(
        outgoing.reshape(n_sub, 1, 2, capacity, width), (n_sub, 2, 2, capacity, width)
    ).reshape(n_within, capacity, width)
    incoming = lax.all_to_all(outgoing, within, 0, 0, tiled=True)
    flat_rows = incoming.reshape(-1, width)
    both = jnp.dot(flat_rows, expert_gate_up, preferred_element_type=jnp.float32)
    units = (jax.nn.silu(both[:, :ff_half]) * both[:, ff_half:]).astype(jnp.bfloat16)
    produced_first = jnp.dot(
        units[:, :ff_quarter], down_first, preferred_element_type=jnp.float32
    ).astype(jnp.bfloat16)
    produced_second = jnp.dot(
        units[:, ff_quarter:], down_second, preferred_element_type=jnp.float32
    ).astype(jnp.bfloat16)
    half_sum = (produced_first.astype(jnp.float32) + produced_second.astype(jnp.float32)).astype(
        jnp.bfloat16
    )
    returned = lax.all_to_all(
        half_sum.reshape(n_within, capacity, width), within, 0, 0, tiled=True
    ).reshape(n_sub, 2, 2, capacity, width)
    expert_out = (returned[:, 0].astype(jnp.float32) + returned[:, 1].astype(jnp.float32)).astype(
        jnp.bfloat16
    )
    expert_out = expert_out.reshape(half_experts * capacity, width)
    pair_out = expert_out[jnp.minimum(target, half_experts * capacity - 1)]
    pair_gates = jnp.where(local_pair, both_gates.reshape(-1), 0.0)
    partial = jnp.sum(
        (pair_gates[:, None] * pair_out.astype(jnp.float32)).reshape(row_count, TOPK, width),
        axis=1,
    )
    combined = jnp.sum(
        lax.all_to_all(partial.reshape(n_zh, quarter, width), "zh", 0, 0, tiled=True), axis=0
    )
    own_places = tp_place * quarter + jnp.arange(quarter)
    live_rows = own_places < prompt_length
    hidden_leaving = jnp.where(live_rows[:, None], after_attn + combined, 0.0).astype(jnp.bfloat16)
    live = (positions < prompt_length)[:, None, None]
    zero_value = jnp.zeros((), jnp.bfloat16)
    keys_kept = jnp.where(live, keys_rotated, zero_value)
    values_kept = jnp.where(live, values_local_rows, zero_value)
    pages_here = column_span // PAGE_POSITIONS
    prompt_pages = jnp.stack([keys_kept, values_kept], axis=1)
    prompt_pages = prompt_pages.reshape(
        pages_here, PAGE_POSITIONS, 2, key_value_local, HEAD_SIZE
    ).transpose(0, 2, 3, 1, 4)
    paged_cache = jnp.zeros(
        (2 * pages_here, 2, key_value_local, PAGE_POSITIONS, HEAD_SIZE), jnp.bfloat16
    )
    paged_cache = paged_cache.at[page_table[0]].set(prompt_pages)
    return (hidden_leaving, paged_cache)


def solution(mesh):
    n_seq, n_tp = mesh.devices.shape
    n_zh = 2
    n_sub = n_seq // n_zh
    split_mesh = Mesh(mesh.devices.reshape(n_zh, n_sub, n_tp), ("zh", "sub", "tp"))
    rows = ("zh", "sub", "tp")
    seq = ("zh", "sub")
    return jax.shard_map(
        functools.partial(on_device, n_zh=n_zh, n_sub=n_sub, n_tp=n_tp),
        mesh=split_mesh,
        in_specs=(
            P(rows, None),
            P(),
            P(rows, None),
            P(),
            P(),
            P("tp", None),
            P(),
            P(),
            P(None, rows, None),
            P(seq, "tp", None),
            P(rows, None),
            P(seq),
            P(seq, None),
        ),
        out_specs=(P(rows, None), P(seq, None, "tp", None, None)),
        check_vma=False,
    )
```

```python
import functools
import math

import jax
import jax.numpy as jnp
from jax import lax
from jax.sharding import Mesh, PartitionSpec as P

QUERY_HEADS = 32
KEY_VALUE_HEADS = 4
HEAD_SIZE = 128
FF = 768
TOPK = 8
PAGE_POSITIONS = 128


EPS = 1e-06
THETA = 1000000.0


def laid_out(pieces, dim):
    pieces = jnp.moveaxis(pieces, 0, dim)
    lengths = pieces.shape
    return pieces.reshape(*lengths[:dim], lengths[dim] * lengths[dim + 1], *lengths[dim + 2 :])


def from_everyone(array, axis):
    peers = lax.axis_size(axis)
    return lax.all_to_all(
        jnp.broadcast_to(array[None], (peers, *array.shape)), axis, 0, 0, tiled=True
    )


def collect(array, axis, dim):
    return laid_out(from_everyone(array, axis), dim)


def in_blocks(array, dim, peers):
    lengths = array.shape
    pieces = array.reshape(*lengths[:dim], peers, lengths[dim] // peers, *lengths[dim + 1 :])
    return jnp.moveaxis(pieces, dim, 0)


def summed_on_arrival(array, axis, dim):
    peers = lax.axis_size(axis)
    pieces = lax.all_to_all(in_blocks(array, dim, peers), axis, 0, 0, tiled=True)
    return jnp.sum(pieces.astype(jnp.float32), axis=0)


def rms_scale(values, gain):
    return values * lax.rsqrt(jnp.mean(values * values, axis=-1, keepdims=True) + EPS) * gain


def rotate(values, positions):
    half_dim = values.shape[-1] // 2
    frequency = THETA ** (-2.0 * jnp.arange(half_dim, dtype=jnp.float32) / values.shape[-1])
    angles = positions.astype(jnp.float32)[:, None] * frequency[None, :]
    cosine = jnp.cos(angles)[:, None, :]
    sine = jnp.sin(angles)[:, None, :]
    first_half = values[..., :half_dim]
    second_half = values[..., half_dim:]
    return jnp.concatenate(
        [first_half * cosine - second_half * sine, second_half * cosine + first_half * sine],
        axis=-1,
    )


def attend_prompt(query_rows, keys_rotated, values_in, prompt_length):
    column_span = query_rows.shape[0]
    scores = jnp.einsum(
        "qhgd,khd->hgqk", query_rows, keys_rotated, preferred_element_type=jnp.float32
    ) / math.sqrt(query_rows.shape[-1])
    places = jnp.arange(column_span)
    allowed = (places[None, :] <= places[:, None]) & (places[None, :] < prompt_length)
    weights = jnp.where(allowed, jnp.exp(scores), 0.0)
    probs = (weights / jnp.sum(weights, axis=-1, keepdims=True)).astype(jnp.bfloat16)
    context_rows = jnp.einsum(
        "hgqk,khd->qhgd", probs, values_in, preferred_element_type=jnp.float32
    )
    return context_rows.astype(jnp.bfloat16).reshape(column_span, -1)


def regroup(features, seq_count, tensor_parallel_count):
    leading = features.shape[:-1]
    blocks = features.reshape(leading + (seq_count, tensor_parallel_count, -1))
    return jnp.swapaxes(blocks, -3, -2).reshape(leading + (-1,))


def on_device(
    hidden_in,
    attention_gain,
    attention_trainer_copy,
    query_gain,
    key_gain,
    output_proj,
    post_gain,
    router_weight,
    gate_up_master,
    down_weight,
    routes,
    lengths,
    page_table,
    *,
    n_zh,
    n_sub,
    n_core,
    n_tp,
):
    zh = lax.axis_index("zh")
    core = lax.axis_index("core")
    tp_place = lax.axis_index("tp")
    everyone = ("zh", "sub2", "core", "tp")
    group = ("sub2", "tp")
    n_group = n_sub * n_tp
    quarter = hidden_in.shape[0]
    width = hidden_in.shape[1]
    experts_all = router_weight.shape[1]
    half_experts = experts_all // n_zh
    heads_here = QUERY_HEADS // n_tp
    key_value_local = KEY_VALUE_HEADS // n_tp
    ff_quarter = FF // n_tp
    capacity = 16

    def flat(a, b, c, d):
        return ((a * n_sub + b) * n_core + c) * n_tp + d

    primary = (tp_place % 2) == core
    slots = [lax.dynamic_index_in_dim(down_weight, tp_place // 2, 0, keepdims=False)]
    for shift in range(1, n_tp):
        pairs = []
        for a in range(n_zh):
            for b in range(n_sub):
                for c in range(n_core):
                    for q in range(n_tp):
                        dest = (q - shift) % n_tp
                        if dest % 2 == c:
                            pairs.append((flat(a, b, c, q), flat(a, b, c, dest)))
        sent = lax.dynamic_index_in_dim(
            down_weight, ((tp_place - shift) % n_tp) // 2, 0, keepdims=False
        )
        slots.append(lax.ppermute(sent, everyone, perm=pairs))
    slots = jnp.stack(slots)
    share = []
    for a in range(n_zh):
        for b in range(n_sub):
            for d in range(n_tp):
                share.append((flat(a, b, d % 2, d), flat(a, b, 1 - d % 2, d)))
    slots = jnp.where(primary, slots, lax.ppermute(slots, everyone, perm=share))

    trainer_block = gate_up_master.shape[1]
    gate_up_half = gate_up_master.astype(jnp.bfloat16).reshape(
        n_zh, half_experts, trainer_block, 2 * FF
    )
    gate_up_half = lax.all_to_all(gate_up_half, "zh", 0, 0, tiled=True)
    pieces = gate_up_half.reshape(n_zh, n_sub, n_tp, trainer_block, n_core, FF)
    pieces = jnp.stack([pieces[:, :, 2 * (d % 2) + d // 2] for d in range(n_tp)], axis=2)
    pieces = pieces.transpose(1, 4, 2, 0, 3, 5).reshape(n_sub * n_core * n_tp, -1, FF)
    pieces = lax.all_to_all(pieces, ("sub2", "core", "tp"), 0, 0, tiled=True)
    column_half = (
        pieces.reshape(n_sub, n_core, n_tp, n_zh, trainer_block, FF)
        .transpose(3, 0, 1, 2, 4, 5)
        .reshape(-1, FF)
    )
    expert_gate_up = lax.all_gather(column_half, "core", axis=1, tiled=True)

    prompt_rows = lax.all_gather(hidden_in, "tp", axis=0, tiled=True)
    column_span = prompt_rows.shape[0]
    normed = rms_scale(prompt_rows.astype(jnp.float32), attention_gain).astype(jnp.bfloat16)
    trainer_rows = attention_trainer_copy.shape[0]
    query_cols = attention_trainer_copy[:, : QUERY_HEADS * HEAD_SIZE].reshape(
        trainer_rows, n_tp, heads_here * HEAD_SIZE
    )
    key_columns = attention_trainer_copy[
        :, QUERY_HEADS * HEAD_SIZE : (QUERY_HEADS + KEY_VALUE_HEADS) * HEAD_SIZE
    ].reshape(trainer_rows, n_tp, key_value_local * HEAD_SIZE)
    value_columns = attention_trainer_copy[
        :, (QUERY_HEADS + KEY_VALUE_HEADS) * HEAD_SIZE :
    ].reshape(trainer_rows, n_tp, key_value_local * HEAD_SIZE)
    joined = (
        jnp.concatenate([query_cols, key_columns, value_columns], axis=2)
        .reshape(trainer_rows, -1)
        .astype(jnp.bfloat16)
    )
    head_rows = lax.all_to_all(joined, "tp", split_axis=1, concat_axis=0, tiled=True)
    head_rows = lax.all_gather(head_rows, "zh", axis=0, tiled=True)
    head_rows = lax.all_gather(head_rows, "sub2", axis=0, tiled=True)
    head_rows = lax.all_gather(head_rows, "core", axis=0, tiled=True)
    seq_block = head_rows.shape[0] // (n_zh * n_sub * n_core)
    normed_order = (
        normed.reshape(column_span, n_zh, n_sub, n_core, seq_block)
        .transpose(0, 3, 2, 1, 4)
        .reshape(column_span, -1)
    )
    projected_rows = jnp.dot(normed_order, head_rows, preferred_element_type=jnp.float32)
    positions = jnp.arange(column_span)
    query_rows = projected_rows[:, : heads_here * HEAD_SIZE].reshape(
        column_span, heads_here, HEAD_SIZE
    )
    keys_raw = projected_rows[
        :, heads_here * HEAD_SIZE : (heads_here + key_value_local) * HEAD_SIZE
    ].reshape(column_span, key_value_local, HEAD_SIZE)
    values_local_rows = (
        projected_rows[:, (heads_here + key_value_local) * HEAD_SIZE :]
        .reshape(column_span, key_value_local, HEAD_SIZE)
        .astype(jnp.bfloat16)
    )
    query_rows = rotate(rms_scale(query_rows, query_gain), positions).astype(jnp.bfloat16)
    keys_rotated = rotate(rms_scale(keys_raw, key_gain), positions).astype(jnp.bfloat16)
    prompt_length = lengths[0]
    context_rows = attend_prompt(
        query_rows.reshape(column_span, key_value_local, QUERY_HEADS // KEY_VALUE_HEADS, HEAD_SIZE),
        keys_rotated,
        values_local_rows,
        prompt_length,
    )
    attention_sums = summed_on_arrival(
        jnp.dot(context_rows, output_proj, preferred_element_type=jnp.float32).astype(jnp.bfloat16),
        "tp",
        0,
    )
    after_attn = hidden_in.astype(jnp.float32) + attention_sums
    mixed = rms_scale(after_attn, post_gain).astype(jnp.bfloat16)

    both_routes = lax.all_gather(routes, "zh", axis=0, tiled=True)
    both_rows = lax.all_gather(mixed, "zh", axis=0, tiled=True)
    row_count = both_rows.shape[0]
    logits = jnp.dot(both_rows, router_weight, preferred_element_type=jnp.float32)
    chosen = jnp.take_along_axis(logits, both_routes, axis=1)
    raised = jnp.exp(chosen)
    gates = raised / jnp.sum(raised, axis=1, keepdims=True)
    pair_expert = both_routes.reshape(-1)
    local_pair = (pair_expert // half_experts) == zh
    local_expert = pair_expert % half_experts
    within_line = local_expert % n_tp
    place = (local_expert // n_tp) * n_tp + 2 * (within_line % 2) + within_line // 2
    hits = (
        (place[:, None] == jnp.arange(half_experts, dtype=jnp.int32)[None, :])
        & local_pair[:, None]
    ).astype(jnp.int32)
    before = jnp.cumsum(hits, axis=0) - hits
    slot_index = jnp.sum(before * hits, axis=1)
    target = jnp.where(local_pair, place * capacity + slot_index, half_experts * capacity)
    outgoing = (
        jnp.zeros((half_experts * capacity, width), jnp.bfloat16)
        .at[target]
        .set(jnp.repeat(both_rows, TOPK, axis=0), mode="drop")
    )
    incoming = lax.all_to_all(
        outgoing.reshape(n_group, capacity, width), group, 0, 0, tiled=True
    )
    flat_rows = incoming.reshape(-1, width)
    both = jnp.dot(flat_rows, expert_gate_up, preferred_element_type=jnp.float32)
    units = (jax.nn.silu(both[:, :FF]) * both[:, FF:]).astype(jnp.bfloat16)
    summed = jnp.zeros((flat_rows.shape[0], width), jnp.float32)
    for slot in range(n_tp):
        lower = ((tp_place + slot) % n_tp) * ff_quarter
        block = lax.dynamic_slice_in_dim(units, lower, ff_quarter, axis=1)
        produced = jnp.dot(block, slots[slot], preferred_element_type=jnp.float32)
        summed = summed + lax.optimization_barrier(produced.astype(jnp.bfloat16)).astype(
            jnp.float32
        )
    expert_result = summed.astype(jnp.bfloat16).reshape(n_group, capacity, width)
    returned = lax.all_to_all(expert_result, group, 0, 0, tiled=True)
    pair_out = returned.reshape(half_experts * capacity, width)[
        jnp.minimum(target, half_experts * capacity - 1)
    ]
    pair_gates = jnp.where(local_pair, gates.reshape(-1), 0.0)
    partial = jnp.sum(
        (pair_gates[:, None] * pair_out.astype(jnp.float32)).reshape(row_count, TOPK, width),
        axis=1,
    )
    combined = jnp.sum(
        lax.all_to_all(partial.reshape(n_zh, quarter, width), "zh", 0, 0, tiled=True), axis=0
    )
    own_places = tp_place * quarter + jnp.arange(quarter)
    live_rows = own_places < prompt_length
    hidden_leaving = jnp.where(live_rows[:, None], after_attn + combined, 0.0).astype(jnp.bfloat16)
    live = (positions < prompt_length)[:, None, None]
    zero_value = jnp.zeros((), jnp.bfloat16)
    keys_kept = jnp.where(live, keys_rotated, zero_value)
    values_kept = jnp.where(live, values_local_rows, zero_value)
    pages_here = column_span // PAGE_POSITIONS
    prompt_pages = jnp.stack([keys_kept, values_kept], axis=1)
    prompt_pages = prompt_pages.reshape(
        pages_here, PAGE_POSITIONS, 2, key_value_local, HEAD_SIZE
    ).transpose(0, 2, 3, 1, 4)
    paged_cache = jnp.zeros(
        (2 * pages_here, 2, key_value_local, PAGE_POSITIONS, HEAD_SIZE), jnp.bfloat16
    )
    paged_cache = paged_cache.at[page_table[0]].set(prompt_pages)
    return (hidden_leaving, paged_cache)


def solution(mesh):
    n_seq, n_tp = mesh.devices.shape
    n_zh = 2
    n_core = 2
    n_sub = n_seq // (n_zh * n_core)
    split_mesh = Mesh(
        mesh.devices.reshape(n_zh, n_sub, n_core, n_tp), ("zh", "sub2", "core", "tp")
    )
    rows = ("zh", "sub2", "core", "tp")
    seq = ("zh", "sub2", "core")
    return jax.shard_map(
        functools.partial(on_device, n_zh=n_zh, n_sub=n_sub, n_core=n_core, n_tp=n_tp),
        mesh=split_mesh,
        in_specs=(
            P(rows, None),
            P(),
            P(rows, None),
            P(),
            P(),
            P("tp", None),
            P(),
            P(),
            P(None, rows, None),
            P(seq, "tp", None),
            P(rows, None),
            P(seq),
            P(seq, None),
        ),
        out_specs=(P(rows, None), P(seq, None, "tp", None, None)),
        check_vma=False,
    )
```

```python
import functools
import math

import jax
import jax.numpy as jnp
from jax import lax
from jax.sharding import Mesh, PartitionSpec as P

QUERY_HEADS = 32
KEY_VALUE_HEADS = 4
HEAD_SIZE = 128
FF = 768
TOPK = 8
PAGE_POSITIONS = 128


EPS = 1e-06
THETA = 1000000.0


def laid_out(pieces, dim):
    pieces = jnp.moveaxis(pieces, 0, dim)
    lengths = pieces.shape
    return pieces.reshape(*lengths[:dim], lengths[dim] * lengths[dim + 1], *lengths[dim + 2 :])


def from_everyone(array, axis):
    peers = lax.axis_size(axis)
    return lax.all_to_all(
        jnp.broadcast_to(array[None], (peers, *array.shape)), axis, 0, 0, tiled=True
    )


def collect(array, axis, dim):
    return laid_out(from_everyone(array, axis), dim)


def in_blocks(array, dim, peers):
    lengths = array.shape
    pieces = array.reshape(*lengths[:dim], peers, lengths[dim] // peers, *lengths[dim + 1 :])
    return jnp.moveaxis(pieces, dim, 0)


def summed_on_arrival(array, axis, dim):
    peers = lax.axis_size(axis)
    pieces = lax.all_to_all(in_blocks(array, dim, peers), axis, 0, 0, tiled=True)
    return jnp.sum(pieces.astype(jnp.float32), axis=0)


def rms_scale(values, gain):
    return values * lax.rsqrt(jnp.mean(values * values, axis=-1, keepdims=True) + EPS) * gain


def rotate(values, positions):
    half_dim = values.shape[-1] // 2
    frequency = THETA ** (-2.0 * jnp.arange(half_dim, dtype=jnp.float32) / values.shape[-1])
    angles = positions.astype(jnp.float32)[:, None] * frequency[None, :]
    cosine = jnp.cos(angles)[:, None, :]
    sine = jnp.sin(angles)[:, None, :]
    first_half = values[..., :half_dim]
    second_half = values[..., half_dim:]
    return jnp.concatenate(
        [first_half * cosine - second_half * sine, second_half * cosine + first_half * sine],
        axis=-1,
    )


def attend_prompt(query_rows, keys_rotated, values_in, prompt_length):
    column_span = query_rows.shape[0]
    scores = jnp.einsum(
        "qhgd,khd->hgqk", query_rows, keys_rotated, preferred_element_type=jnp.float32
    ) / math.sqrt(query_rows.shape[-1])
    places = jnp.arange(column_span)
    allowed = (places[None, :] <= places[:, None]) & (places[None, :] < prompt_length)
    weights = jnp.where(allowed, jnp.exp(scores), 0.0)
    probs = (weights / jnp.sum(weights, axis=-1, keepdims=True)).astype(jnp.bfloat16)
    context_rows = jnp.einsum(
        "hgqk,khd->qhgd", probs, values_in, preferred_element_type=jnp.float32
    )
    return context_rows.astype(jnp.bfloat16).reshape(column_span, -1)


def regroup(features, seq_count, tensor_parallel_count):
    leading = features.shape[:-1]
    blocks = features.reshape(leading + (seq_count, tensor_parallel_count, -1))
    return jnp.swapaxes(blocks, -3, -2).reshape(leading + (-1,))


def on_device(
    hidden_in,
    attention_gain,
    attention_trainer_copy,
    query_gain,
    key_gain,
    output_proj,
    post_gain,
    router_weight,
    gate_up_master,
    down_weight,
    routes,
    lengths,
    page_table,
    *,
    n_zh,
    n_sub,
    n_core,
    n_tp,
):
    zh = lax.axis_index("zh")
    core = lax.axis_index("core")
    tp_place = lax.axis_index("tp")
    everyone = ("zh", "sub2", "core", "tp")
    group = ("sub2", "tp")
    n_group = n_sub * n_tp
    quarter = hidden_in.shape[0]
    width = hidden_in.shape[1]
    experts_all = router_weight.shape[1]
    half_experts = experts_all // n_zh
    heads_here = QUERY_HEADS // n_tp
    key_value_local = KEY_VALUE_HEADS // n_tp
    ff_quarter = FF // n_tp
    capacity = 16

    def flat(a, b, c, d):
        return ((a * n_sub + b) * n_core + c) * n_tp + d

    primary = (tp_place % 2) == core
    slots = [lax.dynamic_index_in_dim(down_weight, tp_place // 2, 0, keepdims=False)]
    for shift in range(1, n_tp):
        pairs = []
        for a in range(n_zh):
            for b in range(n_sub):
                for c in range(n_core):
                    for q in range(n_tp):
                        dest = (q - shift) % n_tp
                        if dest % 2 == c:
                            pairs.append((flat(a, b, c, q), flat(a, b, c, dest)))
        sent = lax.dynamic_index_in_dim(
            down_weight, ((tp_place - shift) % n_tp) // 2, 0, keepdims=False
        )
        slots.append(lax.ppermute(sent, everyone, perm=pairs))
    slots = jnp.stack(slots)
    share = []
    for a in range(n_zh):
        for b in range(n_sub):
            for d in range(n_tp):
                share.append((flat(a, b, d % 2, d), flat(a, b, 1 - d % 2, d)))
    slots = jnp.where(primary, slots, lax.ppermute(slots, everyone, perm=share))
    both_routes = lax.all_gather(routes, "zh", axis=0, tiled=True)
    slots, both_routes, hidden_in = lax.optimization_barrier((slots, both_routes, hidden_in))

    trainer_block = gate_up_master.shape[1]
    gate_up_half = gate_up_master.astype(jnp.bfloat16).reshape(
        n_zh, half_experts, trainer_block, 2 * FF
    )
    gate_up_half = lax.all_to_all(gate_up_half, "zh", 0, 0, tiled=True)
    pieces = gate_up_half.reshape(n_zh, n_sub, n_tp, trainer_block, n_core, FF)
    pieces = jnp.stack([pieces[:, :, 2 * (d % 2) + d // 2] for d in range(n_tp)], axis=2)
    pieces = pieces.transpose(1, 4, 2, 0, 3, 5).reshape(n_sub * n_core * n_tp, -1, FF)
    pieces = lax.all_to_all(pieces, ("sub2", "core", "tp"), 0, 0, tiled=True)
    column_half = (
        pieces.reshape(n_sub, n_core, n_tp, n_zh, trainer_block, FF)
        .transpose(3, 0, 1, 2, 4, 5)
        .reshape(-1, FF)
    )
    expert_gate_up = lax.all_gather(column_half, "core", axis=1, tiled=True)

    prompt_rows = lax.all_gather(hidden_in, "tp", axis=0, tiled=True)
    column_span = prompt_rows.shape[0]
    normed = rms_scale(prompt_rows.astype(jnp.float32), attention_gain).astype(jnp.bfloat16)
    trainer_rows = attention_trainer_copy.shape[0]
    query_cols = attention_trainer_copy[:, : QUERY_HEADS * HEAD_SIZE].reshape(
        trainer_rows, n_tp, heads_here * HEAD_SIZE
    )
    key_columns = attention_trainer_copy[
        :, QUERY_HEADS * HEAD_SIZE : (QUERY_HEADS + KEY_VALUE_HEADS) * HEAD_SIZE
    ].reshape(trainer_rows, n_tp, key_value_local * HEAD_SIZE)
    value_columns = attention_trainer_copy[
        :, (QUERY_HEADS + KEY_VALUE_HEADS) * HEAD_SIZE :
    ].reshape(trainer_rows, n_tp, key_value_local * HEAD_SIZE)
    joined = (
        jnp.concatenate([query_cols, key_columns, value_columns], axis=2)
        .reshape(trainer_rows, -1)
        .astype(jnp.bfloat16)
    )
    head_rows = lax.all_to_all(joined, "tp", split_axis=1, concat_axis=0, tiled=True)
    head_rows = lax.all_gather(head_rows, "zh", axis=0, tiled=True)
    head_rows = lax.all_gather(head_rows, "sub2", axis=0, tiled=True)
    head_rows = lax.all_gather(head_rows, "core", axis=0, tiled=True)
    seq_block = head_rows.shape[0] // (n_zh * n_sub * n_core)
    normed_order = (
        normed.reshape(column_span, n_zh, n_sub, n_core, seq_block)
        .transpose(0, 3, 2, 1, 4)
        .reshape(column_span, -1)
    )
    projected_rows = jnp.dot(normed_order, head_rows, preferred_element_type=jnp.float32)
    positions = jnp.arange(column_span)
    query_rows = projected_rows[:, : heads_here * HEAD_SIZE].reshape(
        column_span, heads_here, HEAD_SIZE
    )
    keys_raw = projected_rows[
        :, heads_here * HEAD_SIZE : (heads_here + key_value_local) * HEAD_SIZE
    ].reshape(column_span, key_value_local, HEAD_SIZE)
    values_local_rows = (
        projected_rows[:, (heads_here + key_value_local) * HEAD_SIZE :]
        .reshape(column_span, key_value_local, HEAD_SIZE)
        .astype(jnp.bfloat16)
    )
    query_rows = rotate(rms_scale(query_rows, query_gain), positions).astype(jnp.bfloat16)
    keys_rotated = rotate(rms_scale(keys_raw, key_gain), positions).astype(jnp.bfloat16)
    prompt_length = lengths[0]
    context_rows = attend_prompt(
        query_rows.reshape(column_span, key_value_local, QUERY_HEADS // KEY_VALUE_HEADS, HEAD_SIZE),
        keys_rotated,
        values_local_rows,
        prompt_length,
    )
    attention_sums = summed_on_arrival(
        jnp.dot(context_rows, output_proj, preferred_element_type=jnp.float32).astype(jnp.bfloat16),
        "tp",
        0,
    )
    after_attn = hidden_in.astype(jnp.float32) + attention_sums
    mixed = rms_scale(after_attn, post_gain).astype(jnp.bfloat16)

    both_rows = lax.all_gather(mixed, "zh", axis=0, tiled=True)
    row_count = both_rows.shape[0]
    logits = jnp.dot(both_rows, router_weight, preferred_element_type=jnp.float32)
    chosen = jnp.take_along_axis(logits, both_routes, axis=1)
    raised = jnp.exp(chosen)
    gates = raised / jnp.sum(raised, axis=1, keepdims=True)
    pair_expert = both_routes.reshape(-1)
    local_pair = (pair_expert // half_experts) == zh
    local_expert = pair_expert % half_experts
    within_line = local_expert % n_tp
    place = (local_expert // n_tp) * n_tp + 2 * (within_line % 2) + within_line // 2
    hits = (
        (place[:, None] == jnp.arange(half_experts, dtype=jnp.int32)[None, :])
        & local_pair[:, None]
    ).astype(jnp.int32)
    pair_count = hits.shape[0]
    earlier = (
        jnp.arange(pair_count)[:, None] > jnp.arange(pair_count)[None, :]
    ).astype(jnp.bfloat16)
    before = jnp.dot(earlier, hits.astype(jnp.bfloat16), preferred_element_type=jnp.float32)
    slot_index = jnp.sum(before * hits.astype(jnp.float32), axis=1).astype(jnp.int32)
    target = jnp.where(local_pair, place * capacity + slot_index, half_experts * capacity)
    outgoing = (
        jnp.zeros((half_experts * capacity, width), jnp.bfloat16)
        .at[target]
        .set(jnp.repeat(both_rows, TOPK, axis=0), mode="drop")
    )
    incoming = lax.all_to_all(
        outgoing.reshape(n_group, capacity, width), group, 0, 0, tiled=True
    )
    flat_rows = incoming.reshape(-1, width)
    both = jnp.dot(flat_rows, expert_gate_up, preferred_element_type=jnp.float32)
    units = (jax.nn.silu(both[:, :FF]) * both[:, FF:]).astype(jnp.bfloat16)
    summed = jnp.zeros((flat_rows.shape[0], width), jnp.float32)
    for slot in range(n_tp):
        lower = ((tp_place + slot) % n_tp) * ff_quarter
        block = lax.dynamic_slice_in_dim(units, lower, ff_quarter, axis=1)
        produced = jnp.dot(block, slots[slot], preferred_element_type=jnp.float32)
        summed = summed + lax.optimization_barrier(produced.astype(jnp.bfloat16)).astype(
            jnp.float32
        )
    expert_result = summed.astype(jnp.bfloat16).reshape(n_group, capacity, width)
    returned = lax.all_to_all(expert_result, group, 0, 0, tiled=True)
    pair_out = returned.reshape(half_experts * capacity, width)[
        jnp.minimum(target, half_experts * capacity - 1)
    ]
    pair_gates = jnp.where(local_pair, gates.reshape(-1), 0.0)
    partial = jnp.sum(
        (pair_gates[:, None] * pair_out.astype(jnp.float32)).reshape(row_count, TOPK, width),
        axis=1,
    )
    combined = jnp.sum(
        lax.all_to_all(partial.reshape(n_zh, quarter, width), "zh", 0, 0, tiled=True), axis=0
    )
    own_places = tp_place * quarter + jnp.arange(quarter)
    live_rows = own_places < prompt_length
    hidden_leaving = jnp.where(live_rows[:, None], after_attn + combined, 0.0).astype(jnp.bfloat16)
    live = (positions < prompt_length)[:, None, None]
    zero_value = jnp.zeros((), jnp.bfloat16)
    keys_kept = jnp.where(live, keys_rotated, zero_value)
    values_kept = jnp.where(live, values_local_rows, zero_value)
    pages_here = column_span // PAGE_POSITIONS
    prompt_pages = jnp.stack([keys_kept, values_kept], axis=1)
    prompt_pages = prompt_pages.reshape(
        pages_here, PAGE_POSITIONS, 2, key_value_local, HEAD_SIZE
    ).transpose(0, 2, 3, 1, 4)
    paged_cache = jnp.zeros(
        (2 * pages_here, 2, key_value_local, PAGE_POSITIONS, HEAD_SIZE), jnp.bfloat16
    )
    paged_cache = paged_cache.at[page_table[0]].set(prompt_pages)
    return (hidden_leaving, paged_cache)


def solution(mesh):
    n_seq, n_tp = mesh.devices.shape
    n_zh = 2
    n_core = 2
    n_sub = n_seq // (n_zh * n_core)
    split_mesh = Mesh(
        mesh.devices.reshape(n_zh, n_sub, n_core, n_tp), ("zh", "sub2", "core", "tp")
    )
    rows = ("zh", "sub2", "core", "tp")
    seq = ("zh", "sub2", "core")
    return jax.shard_map(
        functools.partial(on_device, n_zh=n_zh, n_sub=n_sub, n_core=n_core, n_tp=n_tp),
        mesh=split_mesh,
        in_specs=(
            P(rows, None),
            P(),
            P(rows, None),
            P(),
            P(),
            P("tp", None),
            P(),
            P(),
            P(None, rows, None),
            P(seq, "tp", None),
            P(rows, None),
            P(seq),
            P(seq, None),
        ),
        out_specs=(P(rows, None), P(seq, None, "tp", None, None)),
        check_vma=False,
    )
```

```python
import functools
import math

import jax
import jax.numpy as jnp
from jax import lax
from jax.sharding import Mesh, PartitionSpec as P

QUERY_HEADS = 32
KEY_VALUE_HEADS = 4
HEAD_SIZE = 128
FF = 768
TOPK = 8
PAGE_POSITIONS = 128


EPS = 1e-06
THETA = 1000000.0


def laid_out(pieces, dim):
    pieces = jnp.moveaxis(pieces, 0, dim)
    lengths = pieces.shape
    return pieces.reshape(*lengths[:dim], lengths[dim] * lengths[dim + 1], *lengths[dim + 2 :])


def from_everyone(array, axis):
    peers = lax.axis_size(axis)
    return lax.all_to_all(
        jnp.broadcast_to(array[None], (peers, *array.shape)), axis, 0, 0, tiled=True
    )


def collect(array, axis, dim):
    return laid_out(from_everyone(array, axis), dim)


def in_blocks(array, dim, peers):
    lengths = array.shape
    pieces = array.reshape(*lengths[:dim], peers, lengths[dim] // peers, *lengths[dim + 1 :])
    return jnp.moveaxis(pieces, dim, 0)


def summed_on_arrival(array, axis, dim):
    peers = lax.axis_size(axis)
    pieces = lax.all_to_all(in_blocks(array, dim, peers), axis, 0, 0, tiled=True)
    return jnp.sum(pieces.astype(jnp.float32), axis=0)


def rms_scale(values, gain):
    return values * lax.rsqrt(jnp.mean(values * values, axis=-1, keepdims=True) + EPS) * gain


def rotate(values, positions):
    half_dim = values.shape[-1] // 2
    frequency = THETA ** (-2.0 * jnp.arange(half_dim, dtype=jnp.float32) / values.shape[-1])
    angles = positions.astype(jnp.float32)[:, None] * frequency[None, :]
    cosine = jnp.cos(angles)[:, None, :]
    sine = jnp.sin(angles)[:, None, :]
    first_half = values[..., :half_dim]
    second_half = values[..., half_dim:]
    return jnp.concatenate(
        [first_half * cosine - second_half * sine, second_half * cosine + first_half * sine],
        axis=-1,
    )


def attend_prompt(query_rows, keys_rotated, values_in, prompt_length):
    column_span = query_rows.shape[0]
    scores = jnp.einsum(
        "qhgd,khd->hgqk", query_rows, keys_rotated, preferred_element_type=jnp.float32
    ) / math.sqrt(query_rows.shape[-1])
    places = jnp.arange(column_span)
    allowed = (places[None, :] <= places[:, None]) & (places[None, :] < prompt_length)
    weights = jnp.where(allowed, jnp.exp(scores), 0.0)
    probs = (weights / jnp.sum(weights, axis=-1, keepdims=True)).astype(jnp.bfloat16)
    context_rows = jnp.einsum(
        "hgqk,khd->qhgd", probs, values_in, preferred_element_type=jnp.float32
    )
    return context_rows.astype(jnp.bfloat16).reshape(column_span, -1)


def regroup(features, seq_count, tensor_parallel_count):
    leading = features.shape[:-1]
    blocks = features.reshape(leading + (seq_count, tensor_parallel_count, -1))
    return jnp.swapaxes(blocks, -3, -2).reshape(leading + (-1,))


def on_device(
    hidden_in,
    attention_gain,
    attention_trainer_copy,
    query_gain,
    key_gain,
    output_proj,
    post_gain,
    router_weight,
    gate_up_master,
    down_weight,
    routes,
    lengths,
    page_table,
    *,
    n_zh,
    n_sub,
    n_core,
    n_tp,
):
    zh = lax.axis_index("zh")
    core = lax.axis_index("core")
    tp_place = lax.axis_index("tp")
    everyone = ("zh", "sub2", "core", "tp")
    group = ("sub2", "tp")
    n_group = n_sub * n_tp
    quarter = hidden_in.shape[0]
    width = hidden_in.shape[1]
    experts_all = router_weight.shape[1]
    half_experts = experts_all // n_zh
    heads_here = QUERY_HEADS // n_tp
    key_value_local = KEY_VALUE_HEADS // n_tp
    ff_quarter = FF // n_tp
    capacity = 16

    def flat(a, b, c, d):
        return ((a * n_sub + b) * n_core + c) * n_tp + d

    primary = (tp_place % 2) == core
    slots = [lax.dynamic_index_in_dim(down_weight, tp_place // 2, 0, keepdims=False)]
    for shift in range(1, n_tp):
        pairs = []
        for a in range(n_zh):
            for b in range(n_sub):
                for c in range(n_core):
                    for q in range(n_tp):
                        dest = (q - shift) % n_tp
                        if dest % 2 == c:
                            pairs.append((flat(a, b, c, q), flat(a, b, c, dest)))
        sent = lax.dynamic_index_in_dim(
            down_weight, ((tp_place - shift) % n_tp) // 2, 0, keepdims=False
        )
        slots.append(lax.ppermute(sent, everyone, perm=pairs))
    slots = jnp.stack(slots)
    share = []
    for a in range(n_zh):
        for b in range(n_sub):
            for d in range(n_tp):
                share.append((flat(a, b, d % 2, d), flat(a, b, 1 - d % 2, d)))
    slots = jnp.where(primary, slots, lax.ppermute(slots, everyone, perm=share))
    both_routes = lax.all_gather(routes, "zh", axis=0, tiled=True)
    slots, both_routes, hidden_in = lax.optimization_barrier((slots, both_routes, hidden_in))

    trainer_block = gate_up_master.shape[1]
    gate_up_half = gate_up_master.astype(jnp.bfloat16).reshape(
        n_zh, half_experts, trainer_block, 2 * FF
    )
    gate_up_half = lax.all_to_all(gate_up_half, "zh", 0, 0, tiled=True)
    pieces = gate_up_half.reshape(n_zh, n_sub, n_tp, trainer_block, n_core, FF)
    pieces = jnp.stack([pieces[:, :, 2 * (d % 2) + d // 2] for d in range(n_tp)], axis=2)
    pieces = pieces.transpose(1, 4, 2, 0, 3, 5).reshape(n_sub * n_core * n_tp, -1, FF)
    pieces = lax.all_to_all(pieces, ("sub2", "core", "tp"), 0, 0, tiled=True)
    column_half = (
        pieces.reshape(n_sub, n_core, n_tp, n_zh, trainer_block, FF)
        .transpose(3, 0, 1, 2, 4, 5)
        .reshape(-1, FF)
    )
    expert_gate_up = lax.all_gather(column_half, "core", axis=1, tiled=True)

    prompt_rows = lax.all_gather(hidden_in, "tp", axis=0, tiled=True)
    column_span = prompt_rows.shape[0]
    normed = rms_scale(prompt_rows.astype(jnp.float32), attention_gain).astype(jnp.bfloat16)
    expert_gate_up, normed = lax.optimization_barrier((expert_gate_up, normed))
    trainer_rows = attention_trainer_copy.shape[0]
    query_cols = attention_trainer_copy[:, : QUERY_HEADS * HEAD_SIZE].reshape(
        trainer_rows, n_tp, heads_here * HEAD_SIZE
    )
    key_columns = attention_trainer_copy[
        :, QUERY_HEADS * HEAD_SIZE : (QUERY_HEADS + KEY_VALUE_HEADS) * HEAD_SIZE
    ].reshape(trainer_rows, n_tp, key_value_local * HEAD_SIZE)
    value_columns = attention_trainer_copy[
        :, (QUERY_HEADS + KEY_VALUE_HEADS) * HEAD_SIZE :
    ].reshape(trainer_rows, n_tp, key_value_local * HEAD_SIZE)
    joined = (
        jnp.concatenate([query_cols, key_columns, value_columns], axis=2)
        .reshape(trainer_rows, -1)
        .astype(jnp.bfloat16)
    )
    head_rows = lax.all_to_all(joined, "tp", split_axis=1, concat_axis=0, tiled=True)
    head_rows = lax.all_gather(head_rows, "zh", axis=0, tiled=True)
    head_rows = lax.all_gather(head_rows, "sub2", axis=0, tiled=True)
    head_rows = lax.all_gather(head_rows, "core", axis=0, tiled=True)
    seq_block = head_rows.shape[0] // (n_zh * n_sub * n_core)
    normed_order = (
        normed.reshape(column_span, n_zh, n_sub, n_core, seq_block)
        .transpose(0, 3, 2, 1, 4)
        .reshape(column_span, -1)
    )
    projected_rows = jnp.dot(normed_order, head_rows, preferred_element_type=jnp.float32)
    positions = jnp.arange(column_span)
    query_rows = projected_rows[:, : heads_here * HEAD_SIZE].reshape(
        column_span, heads_here, HEAD_SIZE
    )
    keys_raw = projected_rows[
        :, heads_here * HEAD_SIZE : (heads_here + key_value_local) * HEAD_SIZE
    ].reshape(column_span, key_value_local, HEAD_SIZE)
    values_local_rows = (
        projected_rows[:, (heads_here + key_value_local) * HEAD_SIZE :]
        .reshape(column_span, key_value_local, HEAD_SIZE)
        .astype(jnp.bfloat16)
    )
    query_rows = rotate(rms_scale(query_rows, query_gain), positions).astype(jnp.bfloat16)
    keys_rotated = rotate(rms_scale(keys_raw, key_gain), positions).astype(jnp.bfloat16)
    prompt_length = lengths[0]
    context_rows = attend_prompt(
        query_rows.reshape(column_span, key_value_local, QUERY_HEADS // KEY_VALUE_HEADS, HEAD_SIZE),
        keys_rotated,
        values_local_rows,
        prompt_length,
    )
    attention_sums = summed_on_arrival(
        jnp.dot(context_rows, output_proj, preferred_element_type=jnp.float32).astype(jnp.bfloat16),
        "tp",
        0,
    )
    after_attn = hidden_in.astype(jnp.float32) + attention_sums
    mixed = rms_scale(after_attn, post_gain).astype(jnp.bfloat16)

    both_rows = collect(mixed, "zh", 0)
    row_count = both_rows.shape[0]
    logits = jnp.dot(both_rows, router_weight, preferred_element_type=jnp.float32)
    chosen = jnp.take_along_axis(logits, both_routes, axis=1)
    raised = jnp.exp(chosen)
    gates = raised / jnp.sum(raised, axis=1, keepdims=True)
    pair_expert = both_routes.reshape(-1)
    local_pair = (pair_expert // half_experts) == zh
    local_expert = pair_expert % half_experts
    within_line = local_expert % n_tp
    place = (local_expert // n_tp) * n_tp + 2 * (within_line % 2) + within_line // 2
    hits = (
        (place[:, None] == jnp.arange(half_experts, dtype=jnp.int32)[None, :])
        & local_pair[:, None]
    ).astype(jnp.int32)
    pair_count = hits.shape[0]
    earlier = (
        jnp.arange(pair_count)[:, None] > jnp.arange(pair_count)[None, :]
    ).astype(jnp.bfloat16)
    before = jnp.dot(earlier, hits.astype(jnp.bfloat16), preferred_element_type=jnp.float32)
    slot_index = jnp.sum(before * hits.astype(jnp.float32), axis=1).astype(jnp.int32)
    target = jnp.where(local_pair, place * capacity + slot_index, half_experts * capacity)
    outgoing = (
        jnp.zeros((half_experts * capacity, width), jnp.bfloat16)
        .at[target]
        .set(jnp.repeat(both_rows, TOPK, axis=0), mode="drop")
    )
    incoming = lax.all_to_all(
        outgoing.reshape(n_group, capacity, width), group, 0, 0, tiled=True
    )
    flat_rows = incoming.reshape(-1, width)
    both = jnp.dot(flat_rows, expert_gate_up, preferred_element_type=jnp.float32)
    units = (jax.nn.silu(both[:, :FF]) * both[:, FF:]).astype(jnp.bfloat16)
    summed = jnp.zeros((flat_rows.shape[0], width), jnp.float32)
    for slot in range(n_tp):
        lower = ((tp_place + slot) % n_tp) * ff_quarter
        block = lax.dynamic_slice_in_dim(units, lower, ff_quarter, axis=1)
        produced = jnp.dot(block, slots[slot], preferred_element_type=jnp.float32)
        summed = summed + lax.optimization_barrier(produced.astype(jnp.bfloat16)).astype(
            jnp.float32
        )
    expert_result = summed.astype(jnp.bfloat16).reshape(n_group, capacity, width)
    returned = lax.all_to_all(expert_result, group, 0, 0, tiled=True)
    pair_out = returned.reshape(half_experts * capacity, width)[
        jnp.minimum(target, half_experts * capacity - 1)
    ]
    pair_gates = jnp.where(local_pair, gates.reshape(-1), 0.0)
    partial = jnp.sum(
        (pair_gates[:, None] * pair_out.astype(jnp.float32)).reshape(row_count, TOPK, width),
        axis=1,
    )
    combined = jnp.sum(
        lax.all_to_all(partial.reshape(n_zh, quarter, width), "zh", 0, 0, tiled=True), axis=0
    )
    own_places = tp_place * quarter + jnp.arange(quarter)
    live_rows = own_places < prompt_length
    hidden_leaving = jnp.where(live_rows[:, None], after_attn + combined, 0.0).astype(jnp.bfloat16)
    live = (positions < prompt_length)[:, None, None]
    zero_value = jnp.zeros((), jnp.bfloat16)
    keys_kept = jnp.where(live, keys_rotated, zero_value)
    values_kept = jnp.where(live, values_local_rows, zero_value)
    pages_here = column_span // PAGE_POSITIONS
    prompt_pages = jnp.stack([keys_kept, values_kept], axis=1)
    prompt_pages = prompt_pages.reshape(
        pages_here, PAGE_POSITIONS, 2, key_value_local, HEAD_SIZE
    ).transpose(0, 2, 3, 1, 4)
    paged_cache = jnp.zeros(
        (2 * pages_here, 2, key_value_local, PAGE_POSITIONS, HEAD_SIZE), jnp.bfloat16
    )
    paged_cache = paged_cache.at[page_table[0]].set(prompt_pages)
    return (hidden_leaving, paged_cache)


def solution(mesh):
    n_seq, n_tp = mesh.devices.shape
    n_zh = 2
    n_core = 2
    n_sub = n_seq // (n_zh * n_core)
    split_mesh = Mesh(
        mesh.devices.reshape(n_zh, n_sub, n_core, n_tp), ("zh", "sub2", "core", "tp")
    )
    rows = ("zh", "sub2", "core", "tp")
    seq = ("zh", "sub2", "core")
    return jax.shard_map(
        functools.partial(on_device, n_zh=n_zh, n_sub=n_sub, n_core=n_core, n_tp=n_tp),
        mesh=split_mesh,
        in_specs=(
            P(rows, None),
            P(),
            P(rows, None),
            P(),
            P(),
            P("tp", None),
            P(),
            P(),
            P(None, rows, None),
            P(seq, "tp", None),
            P(rows, None),
            P(seq),
            P(seq, None),
        ),
        out_specs=(P(rows, None), P(seq, None, "tp", None, None)),
        check_vma=False,
    )
```

```python
import functools
import math

import jax
import jax.numpy as jnp
from jax import lax
from jax.sharding import Mesh, PartitionSpec as P

QUERY_HEADS = 32
KEY_VALUE_HEADS = 4
HEAD_SIZE = 128
FF = 768
TOPK = 8
PAGE_POSITIONS = 128


EPS = 1e-06
THETA = 1000000.0


def laid_out(pieces, dim):
    pieces = jnp.moveaxis(pieces, 0, dim)
    lengths = pieces.shape
    return pieces.reshape(*lengths[:dim], lengths[dim] * lengths[dim + 1], *lengths[dim + 2 :])


def from_everyone(array, axis):
    peers = lax.axis_size(axis)
    return lax.all_to_all(
        jnp.broadcast_to(array[None], (peers, *array.shape)), axis, 0, 0, tiled=True
    )


def collect(array, axis, dim):
    return laid_out(from_everyone(array, axis), dim)


def in_blocks(array, dim, peers):
    lengths = array.shape
    pieces = array.reshape(*lengths[:dim], peers, lengths[dim] // peers, *lengths[dim + 1 :])
    return jnp.moveaxis(pieces, dim, 0)


def summed_on_arrival(array, axis, dim):
    peers = lax.axis_size(axis)
    pieces = lax.all_to_all(in_blocks(array, dim, peers), axis, 0, 0, tiled=True)
    return jnp.sum(pieces.astype(jnp.float32), axis=0)


def rms_scale(values, gain):
    return values * lax.rsqrt(jnp.mean(values * values, axis=-1, keepdims=True) + EPS) * gain


def rotate(values, positions):
    half_dim = values.shape[-1] // 2
    frequency = THETA ** (-2.0 * jnp.arange(half_dim, dtype=jnp.float32) / values.shape[-1])
    angles = positions.astype(jnp.float32)[:, None] * frequency[None, :]
    cosine = jnp.cos(angles)[:, None, :]
    sine = jnp.sin(angles)[:, None, :]
    first_half = values[..., :half_dim]
    second_half = values[..., half_dim:]
    return jnp.concatenate(
        [first_half * cosine - second_half * sine, second_half * cosine + first_half * sine],
        axis=-1,
    )


def attend_prompt(query_rows, keys_rotated, values_in, prompt_length):
    column_span = query_rows.shape[0]
    scores = jnp.einsum(
        "qhgd,khd->hgqk", query_rows, keys_rotated, preferred_element_type=jnp.float32
    ) / math.sqrt(query_rows.shape[-1])
    places = jnp.arange(column_span)
    allowed = (places[None, :] <= places[:, None]) & (places[None, :] < prompt_length)
    weights = jnp.where(allowed, jnp.exp(scores), 0.0)
    probs = (weights / jnp.sum(weights, axis=-1, keepdims=True)).astype(jnp.bfloat16)
    context_rows = jnp.einsum(
        "hgqk,khd->qhgd", probs, values_in, preferred_element_type=jnp.float32
    )
    return context_rows.astype(jnp.bfloat16).reshape(column_span, -1)


def regroup(features, seq_count, tensor_parallel_count):
    leading = features.shape[:-1]
    blocks = features.reshape(leading + (seq_count, tensor_parallel_count, -1))
    return jnp.swapaxes(blocks, -3, -2).reshape(leading + (-1,))


def on_device(
    hidden_in,
    attention_gain,
    attention_trainer_copy,
    query_gain,
    key_gain,
    output_proj,
    post_gain,
    router_weight,
    gate_up_master,
    down_weight,
    routes,
    lengths,
    page_table,
    *,
    n_zh,
    n_sub,
    n_core,
    n_tp,
):
    zh = lax.axis_index("zh")
    core = lax.axis_index("core")
    tp_place = lax.axis_index("tp")
    everyone = ("zh", "sub2", "core", "tp")
    group = ("sub2", "tp")
    n_group = n_sub * n_tp
    quarter = hidden_in.shape[0]
    width = hidden_in.shape[1]
    experts_all = router_weight.shape[1]
    half_experts = experts_all // n_zh
    heads_here = QUERY_HEADS // n_tp
    key_value_local = KEY_VALUE_HEADS // n_tp
    ff_quarter = FF // n_tp
    capacity = 16

    def flat(a, b, c, d):
        return ((a * n_sub + b) * n_core + c) * n_tp + d

    primary = (tp_place % 2) == core
    slots = [lax.dynamic_index_in_dim(down_weight, tp_place // 2, 0, keepdims=False)]
    for shift in range(1, n_tp):
        pairs = []
        for a in range(n_zh):
            for b in range(n_sub):
                for c in range(n_core):
                    for q in range(n_tp):
                        dest = (q - shift) % n_tp
                        if dest % 2 == c:
                            pairs.append((flat(a, b, c, q), flat(a, b, c, dest)))
        sent = lax.dynamic_index_in_dim(
            down_weight, ((tp_place - shift) % n_tp) // 2, 0, keepdims=False
        )
        slots.append(lax.ppermute(sent, everyone, perm=pairs))
    slots = jnp.stack(slots)
    share = []
    for a in range(n_zh):
        for b in range(n_sub):
            for d in range(n_tp):
                share.append((flat(a, b, d % 2, d), flat(a, b, 1 - d % 2, d)))
    slots = jnp.where(primary, slots, lax.ppermute(slots, everyone, perm=share))
    both_routes = lax.all_gather(routes, "zh", axis=0, tiled=True)
    slots, both_routes, hidden_in = lax.optimization_barrier((slots, both_routes, hidden_in))

    trainer_block = gate_up_master.shape[1]
    gate_up_half = gate_up_master.astype(jnp.bfloat16).reshape(
        n_zh, half_experts, trainer_block, 2 * FF
    )
    gate_up_half = lax.all_to_all(gate_up_half, "zh", 0, 0, tiled=True)
    pieces = gate_up_half.reshape(n_zh, n_sub, n_tp, trainer_block, n_core, FF)
    pieces = jnp.stack([pieces[:, :, 2 * (d % 2) + d // 2] for d in range(n_tp)], axis=2)
    pieces = pieces.transpose(1, 4, 2, 0, 3, 5).reshape(n_sub * n_core * n_tp, -1, FF)
    pieces = lax.all_to_all(pieces, ("sub2", "core", "tp"), 0, 0, tiled=True)
    column_half = (
        pieces.reshape(n_sub, n_core, n_tp, n_zh, trainer_block, FF)
        .transpose(3, 0, 1, 2, 4, 5)
        .reshape(-1, FF)
    )
    expert_gate_up = lax.all_gather(column_half, "core", axis=1, tiled=True)

    prompt_rows = collect(hidden_in, "tp", 0)
    column_span = prompt_rows.shape[0]
    normed = rms_scale(prompt_rows.astype(jnp.float32), attention_gain).astype(jnp.bfloat16)
    trainer_rows = attention_trainer_copy.shape[0]
    query_cols = attention_trainer_copy[:, : QUERY_HEADS * HEAD_SIZE].reshape(
        trainer_rows, n_tp, heads_here * HEAD_SIZE
    )
    key_columns = attention_trainer_copy[
        :, QUERY_HEADS * HEAD_SIZE : (QUERY_HEADS + KEY_VALUE_HEADS) * HEAD_SIZE
    ].reshape(trainer_rows, n_tp, key_value_local * HEAD_SIZE)
    value_columns = attention_trainer_copy[
        :, (QUERY_HEADS + KEY_VALUE_HEADS) * HEAD_SIZE :
    ].reshape(trainer_rows, n_tp, key_value_local * HEAD_SIZE)
    joined = (
        jnp.concatenate([query_cols, key_columns, value_columns], axis=2)
        .reshape(trainer_rows, -1)
        .astype(jnp.bfloat16)
    )
    head_rows = lax.all_to_all(joined, "tp", split_axis=1, concat_axis=0, tiled=True)
    head_rows = lax.all_gather(head_rows, "zh", axis=0, tiled=True)
    head_rows = lax.all_gather(head_rows, "sub2", axis=0, tiled=True)
    head_rows = lax.all_gather(head_rows, "core", axis=0, tiled=True)
    seq_block = head_rows.shape[0] // (n_zh * n_sub * n_core)
    normed_order = (
        normed.reshape(column_span, n_zh, n_sub, n_core, seq_block)
        .transpose(0, 3, 2, 1, 4)
        .reshape(column_span, -1)
    )
    projected_rows = jnp.dot(normed_order, head_rows, preferred_element_type=jnp.float32)
    positions = jnp.arange(column_span)
    query_rows = projected_rows[:, : heads_here * HEAD_SIZE].reshape(
        column_span, heads_here, HEAD_SIZE
    )
    keys_raw = projected_rows[
        :, heads_here * HEAD_SIZE : (heads_here + key_value_local) * HEAD_SIZE
    ].reshape(column_span, key_value_local, HEAD_SIZE)
    values_local_rows = (
        projected_rows[:, (heads_here + key_value_local) * HEAD_SIZE :]
        .reshape(column_span, key_value_local, HEAD_SIZE)
        .astype(jnp.bfloat16)
    )
    query_rows = rotate(rms_scale(query_rows, query_gain), positions).astype(jnp.bfloat16)
    keys_rotated = rotate(rms_scale(keys_raw, key_gain), positions).astype(jnp.bfloat16)
    prompt_length = lengths[0]
    context_rows = attend_prompt(
        query_rows.reshape(column_span, key_value_local, QUERY_HEADS // KEY_VALUE_HEADS, HEAD_SIZE),
        keys_rotated,
        values_local_rows,
        prompt_length,
    )
    attention_sums = summed_on_arrival(
        jnp.dot(context_rows, output_proj, preferred_element_type=jnp.float32).astype(jnp.bfloat16),
        "tp",
        0,
    )
    after_attn = hidden_in.astype(jnp.float32) + attention_sums
    mixed = rms_scale(after_attn, post_gain).astype(jnp.bfloat16)

    both_rows = collect(mixed, "zh", 0)
    row_count = both_rows.shape[0]
    logits = jnp.dot(both_rows, router_weight, preferred_element_type=jnp.float32)
    chosen = jnp.take_along_axis(logits, both_routes, axis=1)
    raised = jnp.exp(chosen)
    gates = raised / jnp.sum(raised, axis=1, keepdims=True)
    pair_expert = both_routes.reshape(-1)
    local_pair = (pair_expert // half_experts) == zh
    local_expert = pair_expert % half_experts
    within_line = local_expert % n_tp
    place = (local_expert // n_tp) * n_tp + 2 * (within_line % 2) + within_line // 2
    hits = (
        (place[:, None] == jnp.arange(half_experts, dtype=jnp.int32)[None, :])
        & local_pair[:, None]
    ).astype(jnp.int32)
    pair_count = hits.shape[0]
    earlier = (
        jnp.arange(pair_count)[:, None] > jnp.arange(pair_count)[None, :]
    ).astype(jnp.bfloat16)
    before = jnp.dot(earlier, hits.astype(jnp.bfloat16), preferred_element_type=jnp.float32)
    slot_index = jnp.sum(before * hits.astype(jnp.float32), axis=1).astype(jnp.int32)
    target = jnp.where(local_pair, place * capacity + slot_index, half_experts * capacity)
    outgoing = (
        jnp.zeros((half_experts * capacity, width), jnp.bfloat16)
        .at[target]
        .set(jnp.repeat(both_rows, TOPK, axis=0), mode="drop")
    )
    incoming = lax.all_to_all(
        outgoing.reshape(n_group, capacity, width), group, 0, 0, tiled=True
    )
    flat_rows = incoming.reshape(-1, width)
    both = jnp.dot(flat_rows, expert_gate_up, preferred_element_type=jnp.float32)
    units = (jax.nn.silu(both[:, :FF]) * both[:, FF:]).astype(jnp.bfloat16)
    summed = jnp.zeros((flat_rows.shape[0], width), jnp.float32)
    for slot in range(n_tp):
        lower = ((tp_place + slot) % n_tp) * ff_quarter
        block = lax.dynamic_slice_in_dim(units, lower, ff_quarter, axis=1)
        produced = jnp.dot(block, slots[slot], preferred_element_type=jnp.float32)
        summed = summed + lax.optimization_barrier(produced.astype(jnp.bfloat16)).astype(
            jnp.float32
        )
    expert_result = summed.astype(jnp.bfloat16).reshape(n_group, capacity, width)
    returned = lax.all_to_all(expert_result, group, 0, 0, tiled=True)
    pair_out = returned.reshape(half_experts * capacity, width)[
        jnp.minimum(target, half_experts * capacity - 1)
    ]
    pair_gates = jnp.where(local_pair, gates.reshape(-1), 0.0)
    partial = jnp.sum(
        (pair_gates[:, None] * pair_out.astype(jnp.float32)).reshape(row_count, TOPK, width),
        axis=1,
    )
    combined = jnp.sum(
        lax.all_to_all(partial.reshape(n_zh, quarter, width), "zh", 0, 0, tiled=True), axis=0
    )
    own_places = tp_place * quarter + jnp.arange(quarter)
    live_rows = own_places < prompt_length
    hidden_leaving = jnp.where(live_rows[:, None], after_attn + combined, 0.0).astype(jnp.bfloat16)
    live = (positions < prompt_length)[:, None, None]
    zero_value = jnp.zeros((), jnp.bfloat16)
    keys_kept = jnp.where(live, keys_rotated, zero_value)
    values_kept = jnp.where(live, values_local_rows, zero_value)
    pages_here = column_span // PAGE_POSITIONS
    prompt_pages = jnp.stack([keys_kept, values_kept], axis=1)
    prompt_pages = prompt_pages.reshape(
        pages_here, PAGE_POSITIONS, 2, key_value_local, HEAD_SIZE
    ).transpose(0, 2, 3, 1, 4)
    paged_cache = jnp.zeros(
        (2 * pages_here, 2, key_value_local, PAGE_POSITIONS, HEAD_SIZE), jnp.bfloat16
    )
    paged_cache = paged_cache.at[page_table[0]].set(prompt_pages)
    return (hidden_leaving, paged_cache)


def solution(mesh):
    n_seq, n_tp = mesh.devices.shape
    n_zh = 2
    n_core = 2
    n_sub = n_seq // (n_zh * n_core)
    split_mesh = Mesh(
        mesh.devices.reshape(n_zh, n_sub, n_core, n_tp), ("zh", "sub2", "core", "tp")
    )
    rows = ("zh", "sub2", "core", "tp")
    seq = ("zh", "sub2", "core")
    return jax.shard_map(
        functools.partial(on_device, n_zh=n_zh, n_sub=n_sub, n_core=n_core, n_tp=n_tp),
        mesh=split_mesh,
        in_specs=(
            P(rows, None),
            P(),
            P(rows, None),
            P(),
            P(),
            P("tp", None),
            P(),
            P(),
            P(None, rows, None),
            P(seq, "tp", None),
            P(rows, None),
            P(seq),
            P(seq, None),
        ),
        out_specs=(P(rows, None), P(seq, None, "tp", None, None)),
        check_vma=False,
    )
```

```python
import functools
import math

import jax
import jax.numpy as jnp
from jax import lax
from jax.sharding import Mesh, PartitionSpec as P

QUERY_HEADS = 32
KEY_VALUE_HEADS = 4
HEAD_SIZE = 128
FF = 768
TOPK = 8
PAGE_POSITIONS = 128


EPS = 1e-06
THETA = 1000000.0


def laid_out(pieces, dim):
    pieces = jnp.moveaxis(pieces, 0, dim)
    lengths = pieces.shape
    return pieces.reshape(*lengths[:dim], lengths[dim] * lengths[dim + 1], *lengths[dim + 2 :])


def from_everyone(array, axis):
    peers = lax.axis_size(axis)
    return lax.all_to_all(
        jnp.broadcast_to(array[None], (peers, *array.shape)), axis, 0, 0, tiled=True
    )


def collect(array, axis, dim):
    return laid_out(from_everyone(array, axis), dim)


def in_blocks(array, dim, peers):
    lengths = array.shape
    pieces = array.reshape(*lengths[:dim], peers, lengths[dim] // peers, *lengths[dim + 1 :])
    return jnp.moveaxis(pieces, dim, 0)


def summed_on_arrival(array, axis, dim):
    peers = lax.axis_size(axis)
    pieces = lax.all_to_all(in_blocks(array, dim, peers), axis, 0, 0, tiled=True)
    return jnp.sum(pieces.astype(jnp.float32), axis=0)


def rms_scale(values, gain):
    return values * lax.rsqrt(jnp.mean(values * values, axis=-1, keepdims=True) + EPS) * gain


def rotate(values, positions):
    half_dim = values.shape[-1] // 2
    frequency = THETA ** (-2.0 * jnp.arange(half_dim, dtype=jnp.float32) / values.shape[-1])
    angles = positions.astype(jnp.float32)[:, None] * frequency[None, :]
    cosine = jnp.cos(angles)[:, None, :]
    sine = jnp.sin(angles)[:, None, :]
    first_half = values[..., :half_dim]
    second_half = values[..., half_dim:]
    return jnp.concatenate(
        [first_half * cosine - second_half * sine, second_half * cosine + first_half * sine],
        axis=-1,
    )


def attend_prompt(query_rows, keys_rotated, values_in, prompt_length):
    column_span = query_rows.shape[0]
    scores = jnp.einsum(
        "qhgd,khd->hgqk", query_rows, keys_rotated, preferred_element_type=jnp.float32
    ) / math.sqrt(query_rows.shape[-1])
    places = jnp.arange(column_span)
    allowed = (places[None, :] <= places[:, None]) & (places[None, :] < prompt_length)
    weights = jnp.where(allowed, jnp.exp(scores), 0.0)
    probs = (weights / jnp.sum(weights, axis=-1, keepdims=True)).astype(jnp.bfloat16)
    context_rows = jnp.einsum(
        "hgqk,khd->qhgd", probs, values_in, preferred_element_type=jnp.float32
    )
    return context_rows.astype(jnp.bfloat16).reshape(column_span, -1)


def regroup(features, seq_count, tensor_parallel_count):
    leading = features.shape[:-1]
    blocks = features.reshape(leading + (seq_count, tensor_parallel_count, -1))
    return jnp.swapaxes(blocks, -3, -2).reshape(leading + (-1,))


def on_device(
    hidden_in,
    attention_gain,
    attention_trainer_copy,
    query_gain,
    key_gain,
    output_proj,
    post_gain,
    router_weight,
    gate_up_master,
    down_weight,
    routes,
    lengths,
    page_table,
    *,
    n_zh,
    n_sub,
    n_core,
    n_tp,
):
    zh = lax.axis_index("zh")
    core = lax.axis_index("core")
    tp_place = lax.axis_index("tp")
    everyone = ("zh", "sub2", "core", "tp")
    group = ("sub2", "tp")
    n_group = n_sub * n_tp
    quarter = hidden_in.shape[0]
    width = hidden_in.shape[1]
    experts_all = router_weight.shape[1]
    half_experts = experts_all // n_zh
    heads_here = QUERY_HEADS // n_tp
    key_value_local = KEY_VALUE_HEADS // n_tp
    ff_quarter = FF // n_tp
    capacity = 16

    def flat(a, b, c, d):
        return ((a * n_sub + b) * n_core + c) * n_tp + d

    primary = (tp_place % 2) == core
    slots = [lax.dynamic_index_in_dim(down_weight, tp_place // 2, 0, keepdims=False)]
    for shift in range(1, n_tp):
        pairs = []
        for a in range(n_zh):
            for b in range(n_sub):
                for c in range(n_core):
                    for q in range(n_tp):
                        dest = (q - shift) % n_tp
                        if dest % 2 == c:
                            pairs.append((flat(a, b, c, q), flat(a, b, c, dest)))
        sent = lax.dynamic_index_in_dim(
            down_weight, ((tp_place - shift) % n_tp) // 2, 0, keepdims=False
        )
        slots.append(lax.ppermute(sent, everyone, perm=pairs))
    slots = jnp.stack(slots)
    share = []
    for a in range(n_zh):
        for b in range(n_sub):
            for d in range(n_tp):
                share.append((flat(a, b, d % 2, d), flat(a, b, 1 - d % 2, d)))
    slots = jnp.where(primary, slots, lax.ppermute(slots, everyone, perm=share))
    both_routes = lax.all_gather(routes, "zh", axis=0, tiled=True)
    trainer_block = gate_up_master.shape[1]
    gate_up_half = gate_up_master.astype(jnp.bfloat16).reshape(
        n_zh, half_experts, trainer_block, 2 * FF
    )
    gate_up_half = lax.all_to_all(gate_up_half, "zh", 0, 0, tiled=True)
    trainer_rows = attention_trainer_copy.shape[0]
    query_cols = attention_trainer_copy[:, : QUERY_HEADS * HEAD_SIZE].reshape(
        trainer_rows, n_tp, heads_here * HEAD_SIZE
    )
    key_columns = attention_trainer_copy[
        :, QUERY_HEADS * HEAD_SIZE : (QUERY_HEADS + KEY_VALUE_HEADS) * HEAD_SIZE
    ].reshape(trainer_rows, n_tp, key_value_local * HEAD_SIZE)
    value_columns = attention_trainer_copy[
        :, (QUERY_HEADS + KEY_VALUE_HEADS) * HEAD_SIZE :
    ].reshape(trainer_rows, n_tp, key_value_local * HEAD_SIZE)
    joined = (
        jnp.concatenate([query_cols, key_columns, value_columns], axis=2)
        .reshape(trainer_rows, -1)
        .astype(jnp.bfloat16)
    )
    head_rows = lax.all_to_all(joined, "tp", split_axis=1, concat_axis=0, tiled=True)
    head_rows = lax.all_gather(head_rows, "zh", axis=0, tiled=True)
    head_rows = lax.all_gather(head_rows, "sub2", axis=0, tiled=True)
    slots, both_routes, gate_up_half, head_rows, hidden_in = lax.optimization_barrier(
        (slots, both_routes, gate_up_half, head_rows, hidden_in)
    )

    pieces = gate_up_half.reshape(n_zh, n_sub, n_tp, trainer_block, n_core, FF)
    pieces = jnp.stack([pieces[:, :, 2 * (d % 2) + d // 2] for d in range(n_tp)], axis=2)
    pieces = pieces.transpose(1, 4, 2, 0, 3, 5).reshape(n_sub * n_core * n_tp, -1, FF)
    pieces = lax.all_to_all(pieces, ("sub2", "core", "tp"), 0, 0, tiled=True)
    column_half = (
        pieces.reshape(n_sub, n_core, n_tp, n_zh, trainer_block, FF)
        .transpose(3, 0, 1, 2, 4, 5)
        .reshape(-1, FF)
    )

    prompt_rows = collect(hidden_in, "tp", 0)
    column_span = prompt_rows.shape[0]
    normed = rms_scale(prompt_rows.astype(jnp.float32), attention_gain).astype(jnp.bfloat16)
    head_rows = lax.all_gather(head_rows, "core", axis=0, tiled=True)
    seq_block = head_rows.shape[0] // (n_zh * n_sub * n_core)
    normed_order = (
        normed.reshape(column_span, n_zh, n_sub, n_core, seq_block)
        .transpose(0, 3, 2, 1, 4)
        .reshape(column_span, -1)
    )
    projected_rows = jnp.dot(normed_order, head_rows, preferred_element_type=jnp.float32)
    positions = jnp.arange(column_span)
    query_rows = projected_rows[:, : heads_here * HEAD_SIZE].reshape(
        column_span, heads_here, HEAD_SIZE
    )
    keys_raw = projected_rows[
        :, heads_here * HEAD_SIZE : (heads_here + key_value_local) * HEAD_SIZE
    ].reshape(column_span, key_value_local, HEAD_SIZE)
    values_local_rows = (
        projected_rows[:, (heads_here + key_value_local) * HEAD_SIZE :]
        .reshape(column_span, key_value_local, HEAD_SIZE)
        .astype(jnp.bfloat16)
    )
    query_rows = rotate(rms_scale(query_rows, query_gain), positions).astype(jnp.bfloat16)
    keys_rotated = rotate(rms_scale(keys_raw, key_gain), positions).astype(jnp.bfloat16)
    prompt_length = lengths[0]
    context_rows = attend_prompt(
        query_rows.reshape(column_span, key_value_local, QUERY_HEADS // KEY_VALUE_HEADS, HEAD_SIZE),
        keys_rotated,
        values_local_rows,
        prompt_length,
    )
    column_half, context_rows = lax.optimization_barrier((column_half, context_rows))
    expert_gate_up = lax.all_gather(column_half, "core", axis=1, tiled=True)
    attention_sums = summed_on_arrival(
        jnp.dot(context_rows, output_proj, preferred_element_type=jnp.float32).astype(jnp.bfloat16),
        "tp",
        0,
    )
    after_attn = hidden_in.astype(jnp.float32) + attention_sums
    mixed = rms_scale(after_attn, post_gain).astype(jnp.bfloat16)

    both_rows = collect(mixed, "zh", 0)
    row_count = both_rows.shape[0]
    logits = jnp.dot(both_rows, router_weight, preferred_element_type=jnp.float32)
    chosen = jnp.take_along_axis(logits, both_routes, axis=1)
    raised = jnp.exp(chosen)
    gates = raised / jnp.sum(raised, axis=1, keepdims=True)
    pair_expert = both_routes.reshape(-1)
    local_pair = (pair_expert // half_experts) == zh
    local_expert = pair_expert % half_experts
    within_line = local_expert % n_tp
    place = (local_expert // n_tp) * n_tp + 2 * (within_line % 2) + within_line // 2
    hits = (
        (place[:, None] == jnp.arange(half_experts, dtype=jnp.int32)[None, :])
        & local_pair[:, None]
    ).astype(jnp.int32)
    pair_count = hits.shape[0]
    earlier = (
        jnp.arange(pair_count)[:, None] > jnp.arange(pair_count)[None, :]
    ).astype(jnp.bfloat16)
    before = jnp.dot(earlier, hits.astype(jnp.bfloat16), preferred_element_type=jnp.float32)
    slot_index = jnp.sum(before * hits.astype(jnp.float32), axis=1).astype(jnp.int32)
    target = jnp.where(local_pair, place * capacity + slot_index, half_experts * capacity)
    outgoing = (
        jnp.zeros((half_experts * capacity, width), jnp.bfloat16)
        .at[target]
        .set(jnp.repeat(both_rows, TOPK, axis=0), mode="drop")
    )
    incoming = lax.all_to_all(
        outgoing.reshape(n_group, capacity, width), group, 0, 0, tiled=True
    )
    flat_rows = incoming.reshape(-1, width)
    both = jnp.dot(flat_rows, expert_gate_up, preferred_element_type=jnp.float32)
    units = (jax.nn.silu(both[:, :FF]) * both[:, FF:]).astype(jnp.bfloat16)
    summed = jnp.zeros((flat_rows.shape[0], width), jnp.float32)
    for slot in range(n_tp):
        lower = ((tp_place + slot) % n_tp) * ff_quarter
        block = lax.dynamic_slice_in_dim(units, lower, ff_quarter, axis=1)
        produced = jnp.dot(block, slots[slot], preferred_element_type=jnp.float32)
        summed = summed + lax.optimization_barrier(produced.astype(jnp.bfloat16)).astype(
            jnp.float32
        )
    expert_result = summed.astype(jnp.bfloat16).reshape(n_group, capacity, width)
    returned = lax.all_to_all(expert_result, group, 0, 0, tiled=True)
    pair_out = returned.reshape(half_experts * capacity, width)[
        jnp.minimum(target, half_experts * capacity - 1)
    ]
    pair_gates = jnp.where(local_pair, gates.reshape(-1), 0.0)
    partial = jnp.sum(
        (pair_gates[:, None] * pair_out.astype(jnp.float32)).reshape(row_count, TOPK, width),
        axis=1,
    )
    combined = jnp.sum(
        lax.all_to_all(partial.reshape(n_zh, quarter, width), "zh", 0, 0, tiled=True), axis=0
    )
    own_places = tp_place * quarter + jnp.arange(quarter)
    live_rows = own_places < prompt_length
    hidden_leaving = jnp.where(live_rows[:, None], after_attn + combined, 0.0).astype(jnp.bfloat16)
    live = (positions < prompt_length)[:, None, None]
    zero_value = jnp.zeros((), jnp.bfloat16)
    keys_kept = jnp.where(live, keys_rotated, zero_value)
    values_kept = jnp.where(live, values_local_rows, zero_value)
    pages_here = column_span // PAGE_POSITIONS
    prompt_pages = jnp.stack([keys_kept, values_kept], axis=1)
    prompt_pages = prompt_pages.reshape(
        pages_here, PAGE_POSITIONS, 2, key_value_local, HEAD_SIZE
    ).transpose(0, 2, 3, 1, 4)
    paged_cache = jnp.zeros(
        (2 * pages_here, 2, key_value_local, PAGE_POSITIONS, HEAD_SIZE), jnp.bfloat16
    )
    paged_cache = paged_cache.at[page_table[0]].set(prompt_pages)
    return (hidden_leaving, paged_cache)


def solution(mesh):
    n_seq, n_tp = mesh.devices.shape
    n_zh = 2
    n_core = 2
    n_sub = n_seq // (n_zh * n_core)
    split_mesh = Mesh(
        mesh.devices.reshape(n_zh, n_sub, n_core, n_tp), ("zh", "sub2", "core", "tp")
    )
    rows = ("zh", "sub2", "core", "tp")
    seq = ("zh", "sub2", "core")
    return jax.shard_map(
        functools.partial(on_device, n_zh=n_zh, n_sub=n_sub, n_core=n_core, n_tp=n_tp),
        mesh=split_mesh,
        in_specs=(
            P(rows, None),
            P(),
            P(rows, None),
            P(),
            P(),
            P("tp", None),
            P(),
            P(),
            P(None, rows, None),
            P(seq, "tp", None),
            P(rows, None),
            P(seq),
            P(seq, None),
        ),
        out_specs=(P(rows, None), P(seq, None, "tp", None, None)),
        check_vma=False,
    )
```

```python
import functools
import math

import jax
import jax.numpy as jnp
from jax import lax
from jax.sharding import Mesh, PartitionSpec as P

QUERY_HEADS = 32
KEY_VALUE_HEADS = 4
HEAD_SIZE = 128
FF = 768
TOPK = 8
PAGE_POSITIONS = 128


EPS = 1e-06
THETA = 1000000.0


def laid_out(pieces, dim):
    pieces = jnp.moveaxis(pieces, 0, dim)
    lengths = pieces.shape
    return pieces.reshape(*lengths[:dim], lengths[dim] * lengths[dim + 1], *lengths[dim + 2 :])


def from_everyone(array, axis):
    peers = lax.axis_size(axis)
    return lax.all_to_all(
        jnp.broadcast_to(array[None], (peers, *array.shape)), axis, 0, 0, tiled=True
    )


def collect(array, axis, dim):
    return laid_out(from_everyone(array, axis), dim)


def in_blocks(array, dim, peers):
    lengths = array.shape
    pieces = array.reshape(*lengths[:dim], peers, lengths[dim] // peers, *lengths[dim + 1 :])
    return jnp.moveaxis(pieces, dim, 0)


def summed_on_arrival(array, axis, dim):
    peers = lax.axis_size(axis)
    pieces = lax.all_to_all(in_blocks(array, dim, peers), axis, 0, 0, tiled=True)
    return jnp.sum(pieces.astype(jnp.float32), axis=0)


def rms_scale(values, gain):
    return values * lax.rsqrt(jnp.mean(values * values, axis=-1, keepdims=True) + EPS) * gain


def rotate(values, positions):
    half_dim = values.shape[-1] // 2
    frequency = THETA ** (-2.0 * jnp.arange(half_dim, dtype=jnp.float32) / values.shape[-1])
    angles = positions.astype(jnp.float32)[:, None] * frequency[None, :]
    cosine = jnp.cos(angles)[:, None, :]
    sine = jnp.sin(angles)[:, None, :]
    first_half = values[..., :half_dim]
    second_half = values[..., half_dim:]
    return jnp.concatenate(
        [first_half * cosine - second_half * sine, second_half * cosine + first_half * sine],
        axis=-1,
    )


def attend_prompt(query_rows, keys_rotated, values_in, prompt_length):
    column_span = query_rows.shape[0]
    scores = jnp.einsum(
        "qhgd,khd->hgqk", query_rows, keys_rotated, preferred_element_type=jnp.float32
    ) / math.sqrt(query_rows.shape[-1])
    places = jnp.arange(column_span)
    allowed = (places[None, :] <= places[:, None]) & (places[None, :] < prompt_length)
    weights = jnp.where(allowed, jnp.exp(scores), 0.0)
    probs = (weights / jnp.sum(weights, axis=-1, keepdims=True)).astype(jnp.bfloat16)
    context_rows = jnp.einsum(
        "hgqk,khd->qhgd", probs, values_in, preferred_element_type=jnp.float32
    )
    return context_rows.astype(jnp.bfloat16).reshape(column_span, -1)


def regroup(features, seq_count, tensor_parallel_count):
    leading = features.shape[:-1]
    blocks = features.reshape(leading + (seq_count, tensor_parallel_count, -1))
    return jnp.swapaxes(blocks, -3, -2).reshape(leading + (-1,))


def on_device(
    hidden_in,
    attention_gain,
    attention_trainer_copy,
    query_gain,
    key_gain,
    output_proj,
    post_gain,
    router_weight,
    gate_up_master,
    down_weight,
    routes,
    lengths,
    page_table,
    *,
    n_zh,
    n_sub,
    n_core,
    n_tp,
):
    zh = lax.axis_index("zh")
    core = lax.axis_index("core")
    tp_place = lax.axis_index("tp")
    everyone = ("zh", "sub2", "core", "tp")
    group = ("sub2", "tp")
    n_group = n_sub * n_tp
    quarter = hidden_in.shape[0]
    width = hidden_in.shape[1]
    experts_all = router_weight.shape[1]
    half_experts = experts_all // n_zh
    heads_here = QUERY_HEADS // n_tp
    key_value_local = KEY_VALUE_HEADS // n_tp
    ff_quarter = FF // n_tp
    capacity = 16

    def flat(a, b, c, d):
        return ((a * n_sub + b) * n_core + c) * n_tp + d

    primary = (tp_place % 2) == core
    slots = [lax.dynamic_index_in_dim(down_weight, tp_place // 2, 0, keepdims=False)]
    for shift in range(1, n_tp):
        pairs = []
        for a in range(n_zh):
            for b in range(n_sub):
                for c in range(n_core):
                    for q in range(n_tp):
                        dest = (q - shift) % n_tp
                        if dest % 2 == c:
                            pairs.append((flat(a, b, c, q), flat(a, b, c, dest)))
        sent = lax.dynamic_index_in_dim(
            down_weight, ((tp_place - shift) % n_tp) // 2, 0, keepdims=False
        )
        slots.append(lax.ppermute(sent, everyone, perm=pairs))
    slots = jnp.stack(slots)
    share = []
    for a in range(n_zh):
        for b in range(n_sub):
            for d in range(n_tp):
                share.append((flat(a, b, d % 2, d), flat(a, b, 1 - d % 2, d)))
    slots = jnp.where(primary, slots, lax.ppermute(slots, everyone, perm=share))
    both_routes = collect(routes, "zh", 0)
    trainer_block = gate_up_master.shape[1]
    gate_up_half = gate_up_master.astype(jnp.bfloat16).reshape(
        n_zh, half_experts, trainer_block, 2 * FF
    )
    gate_up_half = lax.all_to_all(gate_up_half, "zh", 0, 0, tiled=True)
    trainer_rows = attention_trainer_copy.shape[0]
    query_cols = attention_trainer_copy[:, : QUERY_HEADS * HEAD_SIZE].reshape(
        trainer_rows, n_tp, heads_here * HEAD_SIZE
    )
    key_columns = attention_trainer_copy[
        :, QUERY_HEADS * HEAD_SIZE : (QUERY_HEADS + KEY_VALUE_HEADS) * HEAD_SIZE
    ].reshape(trainer_rows, n_tp, key_value_local * HEAD_SIZE)
    value_columns = attention_trainer_copy[
        :, (QUERY_HEADS + KEY_VALUE_HEADS) * HEAD_SIZE :
    ].reshape(trainer_rows, n_tp, key_value_local * HEAD_SIZE)
    joined = (
        jnp.concatenate([query_cols, key_columns, value_columns], axis=2)
        .reshape(trainer_rows, -1)
        .astype(jnp.bfloat16)
    )
    head_rows = lax.all_to_all(joined, "tp", split_axis=1, concat_axis=0, tiled=True)
    head_rows = lax.all_gather(head_rows, "zh", axis=0, tiled=True)
    head_rows = lax.all_gather(head_rows, "sub2", axis=0, tiled=True)
    slots, both_routes, gate_up_half, head_rows, hidden_in = lax.optimization_barrier(
        (slots, both_routes, gate_up_half, head_rows, hidden_in)
    )

    pieces = gate_up_half.reshape(n_zh, n_sub, n_tp, trainer_block, n_core, FF)
    pieces = jnp.stack([pieces[:, :, 2 * (d % 2) + d // 2] for d in range(n_tp)], axis=2)
    pieces = pieces.transpose(1, 4, 2, 0, 3, 5).reshape(n_sub * n_core * n_tp, -1, FF)
    pieces = lax.all_to_all(pieces, ("sub2", "core", "tp"), 0, 0, tiled=True)
    column_half = (
        pieces.reshape(n_sub, n_core, n_tp, n_zh, trainer_block, FF)
        .transpose(3, 0, 1, 2, 4, 5)
        .reshape(-1, FF)
    )

    prompt_rows = collect(hidden_in, "tp", 0)
    column_span = prompt_rows.shape[0]
    normed = rms_scale(prompt_rows.astype(jnp.float32), attention_gain).astype(jnp.bfloat16)
    head_rows = lax.all_gather(head_rows, "core", axis=0, tiled=True)
    seq_block = head_rows.shape[0] // (n_zh * n_sub * n_core)
    normed_order = (
        normed.reshape(column_span, n_zh, n_sub, n_core, seq_block)
        .transpose(0, 3, 2, 1, 4)
        .reshape(column_span, -1)
    )
    projected_rows = jnp.dot(normed_order, head_rows, preferred_element_type=jnp.float32)
    positions = jnp.arange(column_span)
    query_rows = projected_rows[:, : heads_here * HEAD_SIZE].reshape(
        column_span, heads_here, HEAD_SIZE
    )
    keys_raw = projected_rows[
        :, heads_here * HEAD_SIZE : (heads_here + key_value_local) * HEAD_SIZE
    ].reshape(column_span, key_value_local, HEAD_SIZE)
    values_local_rows = (
        projected_rows[:, (heads_here + key_value_local) * HEAD_SIZE :]
        .reshape(column_span, key_value_local, HEAD_SIZE)
        .astype(jnp.bfloat16)
    )
    query_rows = rotate(rms_scale(query_rows, query_gain), positions).astype(jnp.bfloat16)
    keys_rotated = rotate(rms_scale(keys_raw, key_gain), positions).astype(jnp.bfloat16)
    prompt_length = lengths[0]
    context_rows = attend_prompt(
        query_rows.reshape(column_span, key_value_local, QUERY_HEADS // KEY_VALUE_HEADS, HEAD_SIZE),
        keys_rotated,
        values_local_rows,
        prompt_length,
    )
    column_half, context_rows = lax.optimization_barrier((column_half, context_rows))
    expert_gate_up = lax.all_gather(column_half, "core", axis=1, tiled=True)
    attention_sums = summed_on_arrival(
        jnp.dot(context_rows, output_proj, preferred_element_type=jnp.float32).astype(jnp.bfloat16),
        "tp",
        0,
    )
    after_attn = hidden_in.astype(jnp.float32) + attention_sums
    mixed = rms_scale(after_attn, post_gain).astype(jnp.bfloat16)

    both_rows = collect(mixed, "zh", 0)
    row_count = both_rows.shape[0]
    logits = jnp.dot(both_rows, router_weight, preferred_element_type=jnp.float32)
    chosen = jnp.take_along_axis(logits, both_routes, axis=1)
    raised = jnp.exp(chosen)
    gates = raised / jnp.sum(raised, axis=1, keepdims=True)
    pair_expert = both_routes.reshape(-1)
    local_pair = (pair_expert // half_experts) == zh
    local_expert = pair_expert % half_experts
    within_line = local_expert % n_tp
    place = (local_expert // n_tp) * n_tp + 2 * (within_line % 2) + within_line // 2
    hits = (
        (place[:, None] == jnp.arange(half_experts, dtype=jnp.int32)[None, :])
        & local_pair[:, None]
    ).astype(jnp.int32)
    pair_count = hits.shape[0]
    earlier = (
        jnp.arange(pair_count)[:, None] > jnp.arange(pair_count)[None, :]
    ).astype(jnp.bfloat16)
    before = jnp.dot(earlier, hits.astype(jnp.bfloat16), preferred_element_type=jnp.float32)
    slot_index = jnp.sum(before * hits.astype(jnp.float32), axis=1).astype(jnp.int32)
    target = jnp.where(local_pair, place * capacity + slot_index, half_experts * capacity)
    outgoing = (
        jnp.zeros((half_experts * capacity, width), jnp.bfloat16)
        .at[target]
        .set(jnp.repeat(both_rows, TOPK, axis=0), mode="drop")
    )
    incoming = lax.all_to_all(
        outgoing.reshape(n_group, capacity, width), group, 0, 0, tiled=True
    )
    flat_rows = incoming.reshape(-1, width)
    both = jnp.dot(flat_rows, expert_gate_up, preferred_element_type=jnp.float32)
    units = (jax.nn.silu(both[:, :FF]) * both[:, FF:]).astype(jnp.bfloat16)
    summed = jnp.zeros((flat_rows.shape[0], width), jnp.float32)
    for slot in range(n_tp):
        lower = ((tp_place + slot) % n_tp) * ff_quarter
        block = lax.dynamic_slice_in_dim(units, lower, ff_quarter, axis=1)
        produced = jnp.dot(block, slots[slot], preferred_element_type=jnp.float32)
        summed = summed + lax.optimization_barrier(produced.astype(jnp.bfloat16)).astype(
            jnp.float32
        )
    expert_result = summed.astype(jnp.bfloat16).reshape(n_group, capacity, width)
    returned = lax.all_to_all(expert_result, group, 0, 0, tiled=True)
    pair_out = returned.reshape(half_experts * capacity, width)[
        jnp.minimum(target, half_experts * capacity - 1)
    ]
    pair_gates = jnp.where(local_pair, gates.reshape(-1), 0.0)
    partial = jnp.sum(
        (pair_gates[:, None] * pair_out.astype(jnp.float32)).reshape(row_count, TOPK, width),
        axis=1,
    )
    combined = jnp.sum(
        lax.all_to_all(partial.reshape(n_zh, quarter, width), "zh", 0, 0, tiled=True), axis=0
    )
    own_places = tp_place * quarter + jnp.arange(quarter)
    live_rows = own_places < prompt_length
    hidden_leaving = jnp.where(live_rows[:, None], after_attn + combined, 0.0).astype(jnp.bfloat16)
    live = (positions < prompt_length)[:, None, None]
    zero_value = jnp.zeros((), jnp.bfloat16)
    keys_kept = jnp.where(live, keys_rotated, zero_value)
    values_kept = jnp.where(live, values_local_rows, zero_value)
    pages_here = column_span // PAGE_POSITIONS
    prompt_pages = jnp.stack([keys_kept, values_kept], axis=1)
    prompt_pages = prompt_pages.reshape(
        pages_here, PAGE_POSITIONS, 2, key_value_local, HEAD_SIZE
    ).transpose(0, 2, 3, 1, 4)
    paged_cache = jnp.zeros(
        (2 * pages_here, 2, key_value_local, PAGE_POSITIONS, HEAD_SIZE), jnp.bfloat16
    )
    paged_cache = paged_cache.at[page_table[0]].set(prompt_pages)
    return (hidden_leaving, paged_cache)


def solution(mesh):
    n_seq, n_tp = mesh.devices.shape
    n_zh = 2
    n_core = 2
    n_sub = n_seq // (n_zh * n_core)
    split_mesh = Mesh(
        mesh.devices.reshape(n_zh, n_sub, n_core, n_tp), ("zh", "sub2", "core", "tp")
    )
    rows = ("zh", "sub2", "core", "tp")
    seq = ("zh", "sub2", "core")
    return jax.shard_map(
        functools.partial(on_device, n_zh=n_zh, n_sub=n_sub, n_core=n_core, n_tp=n_tp),
        mesh=split_mesh,
        in_specs=(
            P(rows, None),
            P(),
            P(rows, None),
            P(),
            P(),
            P("tp", None),
            P(),
            P(),
            P(None, rows, None),
            P(seq, "tp", None),
            P(rows, None),
            P(seq),
            P(seq, None),
        ),
        out_specs=(P(rows, None), P(seq, None, "tp", None, None)),
        check_vma=False,
    )
```

```python
import functools
import math

import jax
import jax.numpy as jnp
from jax import lax
from jax.sharding import Mesh, PartitionSpec as P

QUERY_HEADS = 32
KEY_VALUE_HEADS = 4
HEAD_SIZE = 128
FF = 768
TOPK = 8
PAGE_POSITIONS = 128


EPS = 1e-06
THETA = 1000000.0


def laid_out(pieces, dim):
    pieces = jnp.moveaxis(pieces, 0, dim)
    lengths = pieces.shape
    return pieces.reshape(*lengths[:dim], lengths[dim] * lengths[dim + 1], *lengths[dim + 2 :])


def from_everyone(array, axis):
    peers = lax.axis_size(axis)
    return lax.all_to_all(
        jnp.broadcast_to(array[None], (peers, *array.shape)), axis, 0, 0, tiled=True
    )


def collect(array, axis, dim):
    return laid_out(from_everyone(array, axis), dim)


def in_blocks(array, dim, peers):
    lengths = array.shape
    pieces = array.reshape(*lengths[:dim], peers, lengths[dim] // peers, *lengths[dim + 1 :])
    return jnp.moveaxis(pieces, dim, 0)


def summed_on_arrival(array, axis, dim):
    peers = lax.axis_size(axis)
    pieces = lax.all_to_all(in_blocks(array, dim, peers), axis, 0, 0, tiled=True)
    return jnp.sum(pieces.astype(jnp.float32), axis=0)


def rms_scale(values, gain):
    return values * lax.rsqrt(jnp.mean(values * values, axis=-1, keepdims=True) + EPS) * gain


def rotate(values, positions):
    half_dim = values.shape[-1] // 2
    frequency = THETA ** (-2.0 * jnp.arange(half_dim, dtype=jnp.float32) / values.shape[-1])
    angles = positions.astype(jnp.float32)[:, None] * frequency[None, :]
    cosine = jnp.cos(angles)[:, None, :]
    sine = jnp.sin(angles)[:, None, :]
    first_half = values[..., :half_dim]
    second_half = values[..., half_dim:]
    return jnp.concatenate(
        [first_half * cosine - second_half * sine, second_half * cosine + first_half * sine],
        axis=-1,
    )


def attend_prompt(query_rows, keys_rotated, values_in, prompt_length):
    column_span = query_rows.shape[0]
    scores = jnp.einsum(
        "qhgd,khd->hgqk", query_rows, keys_rotated, preferred_element_type=jnp.float32
    ) / math.sqrt(query_rows.shape[-1])
    places = jnp.arange(column_span)
    allowed = (places[None, :] <= places[:, None]) & (places[None, :] < prompt_length)
    weights = jnp.where(allowed, jnp.exp(scores), 0.0)
    probs = (weights / jnp.sum(weights, axis=-1, keepdims=True)).astype(jnp.bfloat16)
    context_rows = jnp.einsum(
        "hgqk,khd->qhgd", probs, values_in, preferred_element_type=jnp.float32
    )
    return context_rows.astype(jnp.bfloat16).reshape(column_span, -1)


def regroup(features, seq_count, tensor_parallel_count):
    leading = features.shape[:-1]
    blocks = features.reshape(leading + (seq_count, tensor_parallel_count, -1))
    return jnp.swapaxes(blocks, -3, -2).reshape(leading + (-1,))


def on_device(
    hidden_in,
    attention_gain,
    attention_trainer_copy,
    query_gain,
    key_gain,
    output_proj,
    post_gain,
    router_weight,
    gate_up_master,
    down_weight,
    routes,
    lengths,
    page_table,
    *,
    n_zh,
    n_sub,
    n_core,
    n_tp,
):
    zh = lax.axis_index("zh")
    core = lax.axis_index("core")
    tp_place = lax.axis_index("tp")
    everyone = ("zh", "sub2", "core", "tp")
    group = ("sub2", "tp")
    n_group = n_sub * n_tp
    quarter = hidden_in.shape[0]
    width = hidden_in.shape[1]
    experts_all = router_weight.shape[1]
    half_experts = experts_all // n_zh
    heads_here = QUERY_HEADS // n_tp
    key_value_local = KEY_VALUE_HEADS // n_tp
    ff_quarter = FF // n_tp
    capacity = 16

    def flat(a, b, c, d):
        return ((a * n_sub + b) * n_core + c) * n_tp + d

    primary = (tp_place % 2) == core
    slots = [lax.dynamic_index_in_dim(down_weight, tp_place // 2, 0, keepdims=False)]
    for shift in range(1, n_tp):
        pairs = []
        for a in range(n_zh):
            for b in range(n_sub):
                for c in range(n_core):
                    for q in range(n_tp):
                        dest = (q - shift) % n_tp
                        if dest % 2 == c:
                            pairs.append((flat(a, b, c, q), flat(a, b, c, dest)))
        sent = lax.dynamic_index_in_dim(
            down_weight, ((tp_place - shift) % n_tp) // 2, 0, keepdims=False
        )
        slots.append(lax.ppermute(sent, everyone, perm=pairs))
    slots = jnp.stack(slots)
    share = []
    for a in range(n_zh):
        for b in range(n_sub):
            for d in range(n_tp):
                share.append((flat(a, b, d % 2, d), flat(a, b, 1 - d % 2, d)))
    slots = jnp.where(primary, slots, lax.ppermute(slots, everyone, perm=share))
    both_routes = lax.all_gather(routes, "zh", axis=0, tiled=True)
    slots, both_routes, hidden_in = lax.optimization_barrier((slots, both_routes, hidden_in))

    trainer_block = gate_up_master.shape[1]
    gate_up_half = gate_up_master.astype(jnp.bfloat16).reshape(
        n_zh, half_experts, trainer_block, 2 * FF
    )
    gate_up_half = lax.all_to_all(gate_up_half, "zh", 0, 0, tiled=True)
    pieces = gate_up_half.reshape(n_zh, n_sub, n_tp, trainer_block, n_core, FF)
    pieces = jnp.stack([pieces[:, :, 2 * (d % 2) + d // 2] for d in range(n_tp)], axis=2)
    pieces = pieces.transpose(1, 4, 2, 0, 3, 5).reshape(n_sub * n_core * n_tp, -1, FF)
    pieces = lax.all_to_all(pieces, ("sub2", "core", "tp"), 0, 0, tiled=True)
    column_half = (
        pieces.reshape(n_sub, n_core, n_tp, n_zh, trainer_block, FF)
        .transpose(3, 0, 1, 2, 4, 5)
        .reshape(-1, FF)
    )
    expert_gate_up = lax.all_gather(column_half, "core", axis=1, tiled=True)

    prompt_rows = collect(hidden_in, "tp", 0)
    column_span = prompt_rows.shape[0]
    normed = rms_scale(prompt_rows.astype(jnp.float32), attention_gain).astype(jnp.bfloat16)
    trainer_rows = attention_trainer_copy.shape[0]
    query_cols = attention_trainer_copy[:, : QUERY_HEADS * HEAD_SIZE].reshape(
        trainer_rows, n_tp, heads_here * HEAD_SIZE
    )
    key_columns = attention_trainer_copy[
        :, QUERY_HEADS * HEAD_SIZE : (QUERY_HEADS + KEY_VALUE_HEADS) * HEAD_SIZE
    ].reshape(trainer_rows, n_tp, key_value_local * HEAD_SIZE)
    value_columns = attention_trainer_copy[
        :, (QUERY_HEADS + KEY_VALUE_HEADS) * HEAD_SIZE :
    ].reshape(trainer_rows, n_tp, key_value_local * HEAD_SIZE)
    joined = (
        jnp.concatenate([query_cols, key_columns, value_columns], axis=2)
        .reshape(trainer_rows, -1)
        .astype(jnp.bfloat16)
    )
    head_rows = lax.all_to_all(joined, "tp", split_axis=1, concat_axis=0, tiled=True)
    head_rows = lax.all_gather(head_rows, "zh", axis=0, tiled=True)
    head_rows = lax.all_gather(head_rows, "sub2", axis=0, tiled=True)
    head_rows = lax.all_gather(head_rows, "core", axis=0, tiled=True)
    seq_block = head_rows.shape[0] // (n_zh * n_sub * n_core)
    normed_order = (
        normed.reshape(column_span, n_zh, n_sub, n_core, seq_block)
        .transpose(0, 3, 2, 1, 4)
        .reshape(column_span, -1)
    )
    projected_rows = jnp.dot(normed_order, head_rows, preferred_element_type=jnp.float32)
    positions = jnp.arange(column_span)
    query_rows = projected_rows[:, : heads_here * HEAD_SIZE].reshape(
        column_span, heads_here, HEAD_SIZE
    )
    keys_raw = projected_rows[
        :, heads_here * HEAD_SIZE : (heads_here + key_value_local) * HEAD_SIZE
    ].reshape(column_span, key_value_local, HEAD_SIZE)
    values_local_rows = (
        projected_rows[:, (heads_here + key_value_local) * HEAD_SIZE :]
        .reshape(column_span, key_value_local, HEAD_SIZE)
        .astype(jnp.bfloat16)
    )
    query_rows = rotate(rms_scale(query_rows, query_gain), positions).astype(jnp.bfloat16)
    keys_rotated = rotate(rms_scale(keys_raw, key_gain), positions).astype(jnp.bfloat16)
    prompt_length = lengths[0]
    context_rows = attend_prompt(
        query_rows.reshape(column_span, key_value_local, QUERY_HEADS // KEY_VALUE_HEADS, HEAD_SIZE),
        keys_rotated,
        values_local_rows,
        prompt_length,
    )
    attention_sums = summed_on_arrival(
        jnp.dot(context_rows, output_proj, preferred_element_type=jnp.float32).astype(jnp.bfloat16),
        "tp",
        0,
    )
    after_attn = hidden_in.astype(jnp.float32) + attention_sums
    mixed = rms_scale(after_attn, post_gain).astype(jnp.bfloat16)

    both_rows = collect(mixed, "zh", 0)
    row_count = both_rows.shape[0]
    logits = jnp.dot(both_rows, router_weight, preferred_element_type=jnp.float32)
    chosen = jnp.take_along_axis(logits, both_routes, axis=1)
    raised = jnp.exp(chosen)
    gates = raised / jnp.sum(raised, axis=1, keepdims=True)
    pair_expert = both_routes.reshape(-1)
    local_pair = (pair_expert // half_experts) == zh
    local_expert = pair_expert % half_experts
    within_line = local_expert % n_tp
    place = (local_expert // n_tp) * n_tp + 2 * (within_line % 2) + within_line // 2
    hits = (
        (place[:, None] == jnp.arange(half_experts, dtype=jnp.int32)[None, :])
        & local_pair[:, None]
    ).astype(jnp.int32)
    pair_count = hits.shape[0]
    earlier = (
        jnp.arange(pair_count)[:, None] > jnp.arange(pair_count)[None, :]
    ).astype(jnp.bfloat16)
    before = jnp.dot(earlier, hits.astype(jnp.bfloat16), preferred_element_type=jnp.float32)
    slot_index = jnp.sum(before * hits.astype(jnp.float32), axis=1).astype(jnp.int32)
    target = jnp.where(local_pair, place * capacity + slot_index, half_experts * capacity)
    outgoing = (
        jnp.zeros((half_experts * capacity, width), jnp.bfloat16)
        .at[target]
        .set(jnp.repeat(both_rows, TOPK, axis=0), mode="drop")
    )
    incoming = lax.all_to_all(
        outgoing.reshape(n_group, capacity, width), group, 0, 0, tiled=True
    )
    flat_rows = incoming.reshape(-1, width)
    both = jnp.dot(flat_rows, expert_gate_up, preferred_element_type=jnp.float32)
    units = (jax.nn.silu(both[:, :FF]) * both[:, FF:]).astype(jnp.bfloat16)
    summed = jnp.zeros((flat_rows.shape[0], width), jnp.float32)
    for slot in range(n_tp):
        lower = ((tp_place + slot) % n_tp) * ff_quarter
        block = lax.dynamic_slice_in_dim(units, lower, ff_quarter, axis=1)
        produced = jnp.dot(block, slots[slot], preferred_element_type=jnp.float32)
        summed = summed + lax.optimization_barrier(produced.astype(jnp.bfloat16)).astype(
            jnp.float32
        )
    expert_result = summed.astype(jnp.bfloat16).reshape(n_group, capacity, width)
    returned = lax.all_to_all(expert_result, group, 0, 0, tiled=True)
    returned = returned.reshape(half_experts * capacity, width)
    pair_gates = jnp.where(local_pair, gates.reshape(-1), 0.0).reshape(n_zh, -1)
    pair_target = jnp.minimum(target, half_experts * capacity - 1).reshape(n_zh, -1)

    def gated_sum(owner):
        picked = returned[lax.dynamic_index_in_dim(pair_target, owner, 0, keepdims=False)]
        weights = lax.dynamic_index_in_dim(pair_gates, owner, 0, keepdims=False)
        return jnp.sum(
            (weights[:, None] * picked.astype(jnp.float32)).reshape(quarter, TOPK, width), axis=1
        )

    from_partner = lax.ppermute(
        gated_sum(1 - zh), "zh", perm=[(i, n_zh - 1 - i) for i in range(n_zh)]
    )
    combined = gated_sum(zh) + from_partner
    own_places = tp_place * quarter + jnp.arange(quarter)
    live_rows = own_places < prompt_length
    hidden_leaving = jnp.where(live_rows[:, None], after_attn + combined, 0.0).astype(jnp.bfloat16)
    live = (positions < prompt_length)[:, None, None]
    zero_value = jnp.zeros((), jnp.bfloat16)
    keys_kept = jnp.where(live, keys_rotated, zero_value)
    values_kept = jnp.where(live, values_local_rows, zero_value)
    pages_here = column_span // PAGE_POSITIONS
    prompt_pages = jnp.stack([keys_kept, values_kept], axis=1)
    prompt_pages = prompt_pages.reshape(
        pages_here, PAGE_POSITIONS, 2, key_value_local, HEAD_SIZE
    ).transpose(0, 2, 3, 1, 4)
    paged_cache = jnp.zeros(
        (2 * pages_here, 2, key_value_local, PAGE_POSITIONS, HEAD_SIZE), jnp.bfloat16
    )
    paged_cache = paged_cache.at[page_table[0]].set(prompt_pages)
    return (hidden_leaving, paged_cache)


def solution(mesh):
    n_seq, n_tp = mesh.devices.shape
    n_zh = 2
    n_core = 2
    n_sub = n_seq // (n_zh * n_core)
    split_mesh = Mesh(
        mesh.devices.reshape(n_zh, n_sub, n_core, n_tp), ("zh", "sub2", "core", "tp")
    )
    rows = ("zh", "sub2", "core", "tp")
    seq = ("zh", "sub2", "core")
    return jax.shard_map(
        functools.partial(on_device, n_zh=n_zh, n_sub=n_sub, n_core=n_core, n_tp=n_tp),
        mesh=split_mesh,
        in_specs=(
            P(rows, None),
            P(),
            P(rows, None),
            P(),
            P(),
            P("tp", None),
            P(),
            P(),
            P(None, rows, None),
            P(seq, "tp", None),
            P(rows, None),
            P(seq),
            P(seq, None),
        ),
        out_specs=(P(rows, None), P(seq, None, "tp", None, None)),
        check_vma=False,
    )
```

```python
import functools
import math

import jax
import jax.numpy as jnp
from jax import lax
from jax.sharding import Mesh, PartitionSpec as P

QUERY_HEADS = 32
KEY_VALUE_HEADS = 4
HEAD_SIZE = 128
FF = 768
TOPK = 8
PAGE_POSITIONS = 128


EPS = 1e-06
THETA = 1000000.0


def laid_out(pieces, dim):
    pieces = jnp.moveaxis(pieces, 0, dim)
    lengths = pieces.shape
    return pieces.reshape(*lengths[:dim], lengths[dim] * lengths[dim + 1], *lengths[dim + 2 :])


def from_everyone(array, axis):
    peers = lax.axis_size(axis)
    return lax.all_to_all(
        jnp.broadcast_to(array[None], (peers, *array.shape)), axis, 0, 0, tiled=True
    )


def collect(array, axis, dim):
    return laid_out(from_everyone(array, axis), dim)


def in_blocks(array, dim, peers):
    lengths = array.shape
    pieces = array.reshape(*lengths[:dim], peers, lengths[dim] // peers, *lengths[dim + 1 :])
    return jnp.moveaxis(pieces, dim, 0)


def summed_on_arrival(array, axis, dim):
    peers = lax.axis_size(axis)
    pieces = lax.all_to_all(in_blocks(array, dim, peers), axis, 0, 0, tiled=True)
    return jnp.sum(pieces.astype(jnp.float32), axis=0)


def rms_scale(values, gain):
    return values * lax.rsqrt(jnp.mean(values * values, axis=-1, keepdims=True) + EPS) * gain


def rotate(values, positions):
    half_dim = values.shape[-1] // 2
    frequency = THETA ** (-2.0 * jnp.arange(half_dim, dtype=jnp.float32) / values.shape[-1])
    angles = positions.astype(jnp.float32)[:, None] * frequency[None, :]
    cosine = jnp.cos(angles)[:, None, :]
    sine = jnp.sin(angles)[:, None, :]
    first_half = values[..., :half_dim]
    second_half = values[..., half_dim:]
    return jnp.concatenate(
        [first_half * cosine - second_half * sine, second_half * cosine + first_half * sine],
        axis=-1,
    )


def attend_prompt(query_rows, keys_rotated, values_in, prompt_length):
    column_span = query_rows.shape[0]
    scores = jnp.einsum(
        "qhgd,khd->hgqk", query_rows, keys_rotated, preferred_element_type=jnp.float32
    ) / math.sqrt(query_rows.shape[-1])
    places = jnp.arange(column_span)
    allowed = (places[None, :] <= places[:, None]) & (places[None, :] < prompt_length)
    weights = jnp.where(allowed, jnp.exp(scores), 0.0)
    probs = (weights / jnp.sum(weights, axis=-1, keepdims=True)).astype(jnp.bfloat16)
    context_rows = jnp.einsum(
        "hgqk,khd->qhgd", probs, values_in, preferred_element_type=jnp.float32
    )
    return context_rows.astype(jnp.bfloat16).reshape(column_span, -1)


def regroup(features, seq_count, tensor_parallel_count):
    leading = features.shape[:-1]
    blocks = features.reshape(leading + (seq_count, tensor_parallel_count, -1))
    return jnp.swapaxes(blocks, -3, -2).reshape(leading + (-1,))


def on_device(
    hidden_in,
    attention_gain,
    attention_trainer_copy,
    query_gain,
    key_gain,
    output_proj,
    post_gain,
    router_weight,
    gate_up_master,
    down_weight,
    routes,
    lengths,
    page_table,
    *,
    n_zh,
    n_sub,
    n_core,
    n_tp,
):
    zh = lax.axis_index("zh")
    core = lax.axis_index("core")
    tp_place = lax.axis_index("tp")
    everyone = ("zh", "sub2", "core", "tp")
    group = ("sub2", "tp")
    n_group = n_sub * n_tp
    quarter = hidden_in.shape[0]
    width = hidden_in.shape[1]
    experts_all = router_weight.shape[1]
    half_experts = experts_all // n_zh
    heads_here = QUERY_HEADS // n_tp
    key_value_local = KEY_VALUE_HEADS // n_tp
    ff_quarter = FF // n_tp
    capacity = 16

    def flat(a, b, c, d):
        return ((a * n_sub + b) * n_core + c) * n_tp + d

    primary = (tp_place % 2) == core
    slots = [lax.dynamic_index_in_dim(down_weight, tp_place // 2, 0, keepdims=False)]
    for shift in range(1, n_tp):
        pairs = []
        for a in range(n_zh):
            for b in range(n_sub):
                for c in range(n_core):
                    for q in range(n_tp):
                        dest = (q - shift) % n_tp
                        if dest % 2 == c:
                            pairs.append((flat(a, b, c, q), flat(a, b, c, dest)))
        sent = lax.dynamic_index_in_dim(
            down_weight, ((tp_place - shift) % n_tp) // 2, 0, keepdims=False
        )
        slots.append(lax.ppermute(sent, everyone, perm=pairs))
    slots = jnp.stack(slots)
    share = []
    for a in range(n_zh):
        for b in range(n_sub):
            for d in range(n_tp):
                share.append((flat(a, b, d % 2, d), flat(a, b, 1 - d % 2, d)))
    slots = jnp.where(primary, slots, lax.ppermute(slots, everyone, perm=share))
    both_routes = lax.all_gather(routes, "zh", axis=0, tiled=True)
    slots, both_routes, hidden_in = lax.optimization_barrier((slots, both_routes, hidden_in))

    trainer_block = gate_up_master.shape[1]
    gate_up_half = gate_up_master.astype(jnp.bfloat16).reshape(
        n_zh, half_experts, trainer_block, 2 * FF
    )
    gate_up_half = lax.all_to_all(gate_up_half, "zh", 0, 0, tiled=True)
    pieces = gate_up_half.reshape(n_zh, n_sub, n_tp, trainer_block, n_core, FF)
    pieces = jnp.stack([pieces[:, :, 2 * (d % 2) + d // 2] for d in range(n_tp)], axis=2)
    pieces = pieces.transpose(1, 4, 2, 0, 3, 5).reshape(n_sub * n_core * n_tp, -1, FF)
    pieces = lax.all_to_all(pieces, ("sub2", "core", "tp"), 0, 0, tiled=True)
    column_half = (
        pieces.reshape(n_sub, n_core, n_tp, n_zh, trainer_block, FF)
        .transpose(3, 0, 1, 2, 4, 5)
        .reshape(-1, FF)
    )
    expert_gate_up = lax.all_gather(column_half, "core", axis=1, tiled=True)

    prompt_rows = collect(hidden_in, "tp", 0)
    column_span = prompt_rows.shape[0]
    normed = rms_scale(prompt_rows.astype(jnp.float32), attention_gain).astype(jnp.bfloat16)
    trainer_rows = attention_trainer_copy.shape[0]
    query_cols = attention_trainer_copy[:, : QUERY_HEADS * HEAD_SIZE].reshape(
        trainer_rows, n_tp, heads_here * HEAD_SIZE
    )
    key_columns = attention_trainer_copy[
        :, QUERY_HEADS * HEAD_SIZE : (QUERY_HEADS + KEY_VALUE_HEADS) * HEAD_SIZE
    ].reshape(trainer_rows, n_tp, key_value_local * HEAD_SIZE)
    value_columns = attention_trainer_copy[
        :, (QUERY_HEADS + KEY_VALUE_HEADS) * HEAD_SIZE :
    ].reshape(trainer_rows, n_tp, key_value_local * HEAD_SIZE)
    joined = (
        jnp.concatenate([query_cols, key_columns, value_columns], axis=2)
        .reshape(trainer_rows, -1)
        .astype(jnp.bfloat16)
    )
    head_rows = lax.all_to_all(joined, "tp", split_axis=1, concat_axis=0, tiled=True)
    head_rows = lax.all_gather(head_rows, "zh", axis=0, tiled=True)
    head_rows = lax.all_gather(head_rows, "sub2", axis=0, tiled=True)
    head_rows = lax.all_gather(head_rows, "core", axis=0, tiled=True)
    seq_block = head_rows.shape[0] // (n_zh * n_sub * n_core)
    normed_order = (
        normed.reshape(column_span, n_zh, n_sub, n_core, seq_block)
        .transpose(0, 3, 2, 1, 4)
        .reshape(column_span, -1)
    )
    projected_rows = jnp.dot(normed_order, head_rows, preferred_element_type=jnp.float32)
    positions = jnp.arange(column_span)
    query_rows = projected_rows[:, : heads_here * HEAD_SIZE].reshape(
        column_span, heads_here, HEAD_SIZE
    )
    keys_raw = projected_rows[
        :, heads_here * HEAD_SIZE : (heads_here + key_value_local) * HEAD_SIZE
    ].reshape(column_span, key_value_local, HEAD_SIZE)
    values_local_rows = (
        projected_rows[:, (heads_here + key_value_local) * HEAD_SIZE :]
        .reshape(column_span, key_value_local, HEAD_SIZE)
        .astype(jnp.bfloat16)
    )
    query_rows = rotate(rms_scale(query_rows, query_gain), positions).astype(jnp.bfloat16)
    keys_rotated = rotate(rms_scale(keys_raw, key_gain), positions).astype(jnp.bfloat16)
    prompt_length = lengths[0]
    context_rows = attend_prompt(
        query_rows.reshape(column_span, key_value_local, QUERY_HEADS // KEY_VALUE_HEADS, HEAD_SIZE),
        keys_rotated,
        values_local_rows,
        prompt_length,
    )
    attention_sums = summed_on_arrival(
        jnp.dot(context_rows, output_proj, preferred_element_type=jnp.float32).astype(jnp.bfloat16),
        "tp",
        0,
    )
    after_attn = hidden_in.astype(jnp.float32) + attention_sums
    mixed = rms_scale(after_attn, post_gain).astype(jnp.bfloat16)

    both_rows = collect(mixed, "zh", 0)
    row_count = both_rows.shape[0]
    logits = jnp.dot(both_rows, router_weight, preferred_element_type=jnp.float32)
    chosen = jnp.take_along_axis(logits, both_routes, axis=1)
    raised = jnp.exp(chosen)
    gates = raised / jnp.sum(raised, axis=1, keepdims=True)
    pair_expert = both_routes.reshape(-1)
    local_pair = (pair_expert // half_experts) == zh
    local_expert = pair_expert % half_experts
    within_line = local_expert % n_tp
    place = (local_expert // n_tp) * n_tp + 2 * (within_line % 2) + within_line // 2
    hits = (
        (place[:, None] == jnp.arange(half_experts, dtype=jnp.int32)[None, :])
        & local_pair[:, None]
    ).astype(jnp.int32)
    pair_count = hits.shape[0]
    earlier = (
        jnp.arange(pair_count)[:, None] > jnp.arange(pair_count)[None, :]
    ).astype(jnp.bfloat16)
    before = jnp.dot(earlier, hits.astype(jnp.bfloat16), preferred_element_type=jnp.float32)
    slot_index = jnp.sum(before * hits.astype(jnp.float32), axis=1).astype(jnp.int32)
    target = jnp.where(local_pair, place * capacity + slot_index, half_experts * capacity)
    outgoing = (
        jnp.zeros((half_experts * capacity, width), jnp.bfloat16)
        .at[target]
        .set(jnp.repeat(both_rows, TOPK, axis=0), mode="drop")
    )
    outgoing = outgoing.reshape(n_group, capacity, width)
    chunk = capacity // 2
    returned_parts = []
    for part in range(2):
        incoming = lax.all_to_all(
            outgoing[:, part * chunk : (part + 1) * chunk], group, 0, 0, tiled=True
        )
        flat_rows = incoming.reshape(-1, width)
        both = jnp.dot(flat_rows, expert_gate_up, preferred_element_type=jnp.float32)
        units = (jax.nn.silu(both[:, :FF]) * both[:, FF:]).astype(jnp.bfloat16)
        summed = jnp.zeros((flat_rows.shape[0], width), jnp.float32)
        for slot in range(n_tp):
            lower = ((tp_place + slot) % n_tp) * ff_quarter
            block = lax.dynamic_slice_in_dim(units, lower, ff_quarter, axis=1)
            produced = jnp.dot(block, slots[slot], preferred_element_type=jnp.float32)
            summed = summed + lax.optimization_barrier(produced.astype(jnp.bfloat16)).astype(
                jnp.float32
            )
        expert_result = summed.astype(jnp.bfloat16).reshape(n_group, chunk, width)
        returned_parts.append(lax.all_to_all(expert_result, group, 0, 0, tiled=True))
    returned = jnp.concatenate(returned_parts, axis=1)
    returned = returned.reshape(half_experts * capacity, width)
    pair_gates = jnp.where(local_pair, gates.reshape(-1), 0.0).reshape(n_zh, -1)
    pair_target = jnp.minimum(target, half_experts * capacity - 1).reshape(n_zh, -1)

    def gated_sum(owner):
        picked = returned[lax.dynamic_index_in_dim(pair_target, owner, 0, keepdims=False)]
        weights = lax.dynamic_index_in_dim(pair_gates, owner, 0, keepdims=False)
        return jnp.sum(
            (weights[:, None] * picked.astype(jnp.float32)).reshape(quarter, TOPK, width), axis=1
        )

    from_partner = lax.ppermute(
        gated_sum(1 - zh), "zh", perm=[(i, n_zh - 1 - i) for i in range(n_zh)]
    )
    combined = gated_sum(zh) + from_partner
    own_places = tp_place * quarter + jnp.arange(quarter)
    live_rows = own_places < prompt_length
    hidden_leaving = jnp.where(live_rows[:, None], after_attn + combined, 0.0).astype(jnp.bfloat16)
    live = (positions < prompt_length)[:, None, None]
    zero_value = jnp.zeros((), jnp.bfloat16)
    keys_kept = jnp.where(live, keys_rotated, zero_value)
    values_kept = jnp.where(live, values_local_rows, zero_value)
    pages_here = column_span // PAGE_POSITIONS
    prompt_pages = jnp.stack([keys_kept, values_kept], axis=1)
    prompt_pages = prompt_pages.reshape(
        pages_here, PAGE_POSITIONS, 2, key_value_local, HEAD_SIZE
    ).transpose(0, 2, 3, 1, 4)
    paged_cache = jnp.zeros(
        (2 * pages_here, 2, key_value_local, PAGE_POSITIONS, HEAD_SIZE), jnp.bfloat16
    )
    paged_cache = paged_cache.at[page_table[0]].set(prompt_pages)
    return (hidden_leaving, paged_cache)


def solution(mesh):
    n_seq, n_tp = mesh.devices.shape
    n_zh = 2
    n_core = 2
    n_sub = n_seq // (n_zh * n_core)
    split_mesh = Mesh(
        mesh.devices.reshape(n_zh, n_sub, n_core, n_tp), ("zh", "sub2", "core", "tp")
    )
    rows = ("zh", "sub2", "core", "tp")
    seq = ("zh", "sub2", "core")
    return jax.shard_map(
        functools.partial(on_device, n_zh=n_zh, n_sub=n_sub, n_core=n_core, n_tp=n_tp),
        mesh=split_mesh,
        in_specs=(
            P(rows, None),
            P(),
            P(rows, None),
            P(),
            P(),
            P("tp", None),
            P(),
            P(),
            P(None, rows, None),
            P(seq, "tp", None),
            P(rows, None),
            P(seq),
            P(seq, None),
        ),
        out_specs=(P(rows, None), P(seq, None, "tp", None, None)),
        check_vma=False,
    )
```

```python
import functools
import math

import jax
import jax.numpy as jnp
from jax import lax
from jax.sharding import Mesh, PartitionSpec as P

QUERY_HEADS = 32
KEY_VALUE_HEADS = 4
HEAD_SIZE = 128
FF = 768
TOPK = 8
PAGE_POSITIONS = 128


EPS = 1e-06
THETA = 1000000.0


def laid_out(pieces, dim):
    pieces = jnp.moveaxis(pieces, 0, dim)
    lengths = pieces.shape
    return pieces.reshape(*lengths[:dim], lengths[dim] * lengths[dim + 1], *lengths[dim + 2 :])


def from_everyone(array, axis):
    peers = lax.axis_size(axis)
    return lax.all_to_all(
        jnp.broadcast_to(array[None], (peers, *array.shape)), axis, 0, 0, tiled=True
    )


def collect(array, axis, dim):
    return laid_out(from_everyone(array, axis), dim)


def in_blocks(array, dim, peers):
    lengths = array.shape
    pieces = array.reshape(*lengths[:dim], peers, lengths[dim] // peers, *lengths[dim + 1 :])
    return jnp.moveaxis(pieces, dim, 0)


def summed_on_arrival(array, axis, dim):
    peers = lax.axis_size(axis)
    pieces = lax.all_to_all(in_blocks(array, dim, peers), axis, 0, 0, tiled=True)
    return jnp.sum(pieces.astype(jnp.float32), axis=0)


def rms_scale(values, gain):
    return values * lax.rsqrt(jnp.mean(values * values, axis=-1, keepdims=True) + EPS) * gain


def rotate(values, positions):
    half_dim = values.shape[-1] // 2
    frequency = THETA ** (-2.0 * jnp.arange(half_dim, dtype=jnp.float32) / values.shape[-1])
    angles = positions.astype(jnp.float32)[:, None] * frequency[None, :]
    cosine = jnp.cos(angles)[:, None, :]
    sine = jnp.sin(angles)[:, None, :]
    first_half = values[..., :half_dim]
    second_half = values[..., half_dim:]
    return jnp.concatenate(
        [first_half * cosine - second_half * sine, second_half * cosine + first_half * sine],
        axis=-1,
    )


def attend_prompt(query_rows, keys_rotated, values_in, prompt_length):
    column_span = query_rows.shape[0]
    scores = jnp.einsum(
        "qhgd,khd->hgqk", query_rows, keys_rotated, preferred_element_type=jnp.float32
    ) / math.sqrt(query_rows.shape[-1])
    places = jnp.arange(column_span)
    allowed = (places[None, :] <= places[:, None]) & (places[None, :] < prompt_length)
    weights = jnp.where(allowed, jnp.exp(scores), 0.0)
    probs = (weights / jnp.sum(weights, axis=-1, keepdims=True)).astype(jnp.bfloat16)
    context_rows = jnp.einsum(
        "hgqk,khd->qhgd", probs, values_in, preferred_element_type=jnp.float32
    )
    return context_rows.astype(jnp.bfloat16).reshape(column_span, -1)


def regroup(features, seq_count, tensor_parallel_count):
    leading = features.shape[:-1]
    blocks = features.reshape(leading + (seq_count, tensor_parallel_count, -1))
    return jnp.swapaxes(blocks, -3, -2).reshape(leading + (-1,))


def on_device(
    hidden_in,
    attention_gain,
    attention_trainer_copy,
    query_gain,
    key_gain,
    output_proj,
    post_gain,
    router_weight,
    gate_up_master,
    down_weight,
    routes,
    lengths,
    page_table,
    *,
    n_zh,
    n_sub,
    n_core,
    n_tp,
):
    zh = lax.axis_index("zh")
    core = lax.axis_index("core")
    tp_place = lax.axis_index("tp")
    everyone = ("zh", "sub2", "core", "tp")
    group = ("sub2", "tp")
    n_group = n_sub * n_tp
    quarter = hidden_in.shape[0]
    width = hidden_in.shape[1]
    experts_all = router_weight.shape[1]
    half_experts = experts_all // n_zh
    heads_here = QUERY_HEADS // n_tp
    key_value_local = KEY_VALUE_HEADS // n_tp
    ff_quarter = FF // n_tp
    capacity = 16

    def flat(a, b, c, d):
        return ((a * n_sub + b) * n_core + c) * n_tp + d

    primary = (tp_place % 2) == core
    slots = [lax.dynamic_index_in_dim(down_weight, tp_place // 2, 0, keepdims=False)]
    for shift in range(1, n_tp):
        pairs = []
        for a in range(n_zh):
            for b in range(n_sub):
                for c in range(n_core):
                    for q in range(n_tp):
                        dest = (q - shift) % n_tp
                        if dest % 2 == c:
                            pairs.append((flat(a, b, c, q), flat(a, b, c, dest)))
        sent = lax.dynamic_index_in_dim(
            down_weight, ((tp_place - shift) % n_tp) // 2, 0, keepdims=False
        )
        slots.append(lax.ppermute(sent, everyone, perm=pairs))
    slots = jnp.stack(slots)
    share = []
    for a in range(n_zh):
        for b in range(n_sub):
            for d in range(n_tp):
                share.append((flat(a, b, d % 2, d), flat(a, b, 1 - d % 2, d)))
    slots = jnp.where(primary, slots, lax.ppermute(slots, everyone, perm=share))
    both_routes = lax.all_gather(routes, "zh", axis=0, tiled=True)
    slots, both_routes, hidden_in = lax.optimization_barrier((slots, both_routes, hidden_in))

    trainer_block = gate_up_master.shape[1]
    gate_up_half = gate_up_master.astype(jnp.bfloat16).reshape(
        n_zh, half_experts, trainer_block, 2 * FF
    )
    gate_up_half = lax.all_to_all(gate_up_half, "zh", 0, 0, tiled=True)
    pieces = gate_up_half.reshape(n_zh, n_sub, n_tp, trainer_block, n_core, FF)
    pieces = jnp.stack([pieces[:, :, 2 * (d % 2) + d // 2] for d in range(n_tp)], axis=2)
    pieces = pieces.transpose(1, 4, 2, 0, 3, 5).reshape(n_sub * n_core * n_tp, -1, FF)
    pieces = lax.all_to_all(pieces, ("sub2", "core", "tp"), 0, 0, tiled=True)
    column_half = (
        pieces.reshape(n_sub, n_core, n_tp, n_zh, trainer_block, FF)
        .transpose(3, 0, 1, 2, 4, 5)
        .reshape(-1, FF)
    )

    prompt_rows = collect(hidden_in, "tp", 0)
    column_span = prompt_rows.shape[0]
    normed = rms_scale(prompt_rows.astype(jnp.float32), attention_gain).astype(jnp.bfloat16)
    trainer_rows = attention_trainer_copy.shape[0]
    query_cols = attention_trainer_copy[:, : QUERY_HEADS * HEAD_SIZE].reshape(
        trainer_rows, n_tp, heads_here * HEAD_SIZE
    )
    key_columns = attention_trainer_copy[
        :, QUERY_HEADS * HEAD_SIZE : (QUERY_HEADS + KEY_VALUE_HEADS) * HEAD_SIZE
    ].reshape(trainer_rows, n_tp, key_value_local * HEAD_SIZE)
    value_columns = attention_trainer_copy[
        :, (QUERY_HEADS + KEY_VALUE_HEADS) * HEAD_SIZE :
    ].reshape(trainer_rows, n_tp, key_value_local * HEAD_SIZE)
    joined = (
        jnp.concatenate([query_cols, key_columns, value_columns], axis=2)
        .reshape(trainer_rows, -1)
        .astype(jnp.bfloat16)
    )
    head_rows = lax.all_to_all(joined, "tp", split_axis=1, concat_axis=0, tiled=True)
    head_rows = lax.all_gather(head_rows, "zh", axis=0, tiled=True)
    head_rows = lax.all_gather(head_rows, "sub2", axis=0, tiled=True)
    head_rows = lax.all_gather(head_rows, "core", axis=0, tiled=True)
    seq_block = head_rows.shape[0] // (n_zh * n_sub * n_core)
    normed_order = (
        normed.reshape(column_span, n_zh, n_sub, n_core, seq_block)
        .transpose(0, 3, 2, 1, 4)
        .reshape(column_span, -1)
    )
    projected_rows = jnp.dot(normed_order, head_rows, preferred_element_type=jnp.float32)
    positions = jnp.arange(column_span)
    query_rows = projected_rows[:, : heads_here * HEAD_SIZE].reshape(
        column_span, heads_here, HEAD_SIZE
    )
    keys_raw = projected_rows[
        :, heads_here * HEAD_SIZE : (heads_here + key_value_local) * HEAD_SIZE
    ].reshape(column_span, key_value_local, HEAD_SIZE)
    values_local_rows = (
        projected_rows[:, (heads_here + key_value_local) * HEAD_SIZE :]
        .reshape(column_span, key_value_local, HEAD_SIZE)
        .astype(jnp.bfloat16)
    )
    query_rows = rotate(rms_scale(query_rows, query_gain), positions).astype(jnp.bfloat16)
    keys_rotated = rotate(rms_scale(keys_raw, key_gain), positions).astype(jnp.bfloat16)
    prompt_length = lengths[0]
    context_rows = attend_prompt(
        query_rows.reshape(column_span, key_value_local, QUERY_HEADS // KEY_VALUE_HEADS, HEAD_SIZE),
        keys_rotated,
        values_local_rows,
        prompt_length,
    )
    column_half, context_rows = lax.optimization_barrier((column_half, context_rows))
    expert_gate_up = lax.all_gather(column_half, "core", axis=1, tiled=True)
    attention_sums = summed_on_arrival(
        jnp.dot(context_rows, output_proj, preferred_element_type=jnp.float32).astype(jnp.bfloat16),
        "tp",
        0,
    )
    after_attn = hidden_in.astype(jnp.float32) + attention_sums
    mixed = rms_scale(after_attn, post_gain).astype(jnp.bfloat16)

    both_rows = collect(mixed, "zh", 0)
    row_count = both_rows.shape[0]
    logits = jnp.dot(both_rows, router_weight, preferred_element_type=jnp.float32)
    chosen = jnp.take_along_axis(logits, both_routes, axis=1)
    raised = jnp.exp(chosen)
    gates = raised / jnp.sum(raised, axis=1, keepdims=True)
    pair_expert = both_routes.reshape(-1)
    local_pair = (pair_expert // half_experts) == zh
    local_expert = pair_expert % half_experts
    within_line = local_expert % n_tp
    place = (local_expert // n_tp) * n_tp + 2 * (within_line % 2) + within_line // 2
    hits = (
        (place[:, None] == jnp.arange(half_experts, dtype=jnp.int32)[None, :])
        & local_pair[:, None]
    ).astype(jnp.int32)
    pair_count = hits.shape[0]
    earlier = (
        jnp.arange(pair_count)[:, None] > jnp.arange(pair_count)[None, :]
    ).astype(jnp.bfloat16)
    before = jnp.dot(earlier, hits.astype(jnp.bfloat16), preferred_element_type=jnp.float32)
    slot_index = jnp.sum(before * hits.astype(jnp.float32), axis=1).astype(jnp.int32)
    target = jnp.where(local_pair, place * capacity + slot_index, half_experts * capacity)
    outgoing = (
        jnp.zeros((half_experts * capacity, width), jnp.bfloat16)
        .at[target]
        .set(jnp.repeat(both_rows, TOPK, axis=0), mode="drop")
    )
    incoming = lax.all_to_all(
        outgoing.reshape(n_group, capacity, width), group, 0, 0, tiled=True
    )
    flat_rows = incoming.reshape(-1, width)
    both = jnp.dot(flat_rows, expert_gate_up, preferred_element_type=jnp.float32)
    units = (jax.nn.silu(both[:, :FF]) * both[:, FF:]).astype(jnp.bfloat16)
    summed = jnp.zeros((flat_rows.shape[0], width), jnp.float32)
    for slot in range(n_tp):
        lower = ((tp_place + slot) % n_tp) * ff_quarter
        block = lax.dynamic_slice_in_dim(units, lower, ff_quarter, axis=1)
        produced = jnp.dot(block, slots[slot], preferred_element_type=jnp.float32)
        summed = summed + lax.optimization_barrier(produced.astype(jnp.bfloat16)).astype(
            jnp.float32
        )
    expert_result = summed.astype(jnp.bfloat16).reshape(n_group, capacity, width)
    returned = lax.all_to_all(expert_result, group, 0, 0, tiled=True)
    returned = returned.reshape(half_experts * capacity, width)
    pair_gates = jnp.where(local_pair, gates.reshape(-1), 0.0).reshape(n_zh, -1)
    pair_target = jnp.minimum(target, half_experts * capacity - 1).reshape(n_zh, -1)

    def gated_sum(owner):
        picked = returned[lax.dynamic_index_in_dim(pair_target, owner, 0, keepdims=False)]
        weights = lax.dynamic_index_in_dim(pair_gates, owner, 0, keepdims=False)
        return jnp.sum(
            (weights[:, None] * picked.astype(jnp.float32)).reshape(quarter, TOPK, width), axis=1
        )

    from_partner = lax.ppermute(
        gated_sum(1 - zh), "zh", perm=[(i, n_zh - 1 - i) for i in range(n_zh)]
    )
    combined = gated_sum(zh) + from_partner
    own_places = tp_place * quarter + jnp.arange(quarter)
    live_rows = own_places < prompt_length
    hidden_leaving = jnp.where(live_rows[:, None], after_attn + combined, 0.0).astype(jnp.bfloat16)
    live = (positions < prompt_length)[:, None, None]
    zero_value = jnp.zeros((), jnp.bfloat16)
    keys_kept = jnp.where(live, keys_rotated, zero_value)
    values_kept = jnp.where(live, values_local_rows, zero_value)
    pages_here = column_span // PAGE_POSITIONS
    prompt_pages = jnp.stack([keys_kept, values_kept], axis=1)
    prompt_pages = prompt_pages.reshape(
        pages_here, PAGE_POSITIONS, 2, key_value_local, HEAD_SIZE
    ).transpose(0, 2, 3, 1, 4)
    paged_cache = jnp.zeros(
        (2 * pages_here, 2, key_value_local, PAGE_POSITIONS, HEAD_SIZE), jnp.bfloat16
    )
    paged_cache = paged_cache.at[page_table[0]].set(prompt_pages)
    return (hidden_leaving, paged_cache)


def solution(mesh):
    n_seq, n_tp = mesh.devices.shape
    n_zh = 2
    n_core = 2
    n_sub = n_seq // (n_zh * n_core)
    split_mesh = Mesh(
        mesh.devices.reshape(n_zh, n_sub, n_core, n_tp), ("zh", "sub2", "core", "tp")
    )
    rows = ("zh", "sub2", "core", "tp")
    seq = ("zh", "sub2", "core")
    return jax.shard_map(
        functools.partial(on_device, n_zh=n_zh, n_sub=n_sub, n_core=n_core, n_tp=n_tp),
        mesh=split_mesh,
        in_specs=(
            P(rows, None),
            P(),
            P(rows, None),
            P(),
            P(),
            P("tp", None),
            P(),
            P(),
            P(None, rows, None),
            P(seq, "tp", None),
            P(rows, None),
            P(seq),
            P(seq, None),
        ),
        out_specs=(P(rows, None), P(seq, None, "tp", None, None)),
        check_vma=False,
    )
```
